512 devices in a mesh: seq: 64 (over z, y), dp: 8 (over x, core).
Axes of the slice: x: 4, y: 8, z: 8, core: 2. Of those that a mesh axis runs over, the one named last changes fastest.
Arguments:
- queries: bfloat16 [8192, 2048], P('seq', 'dp'), may hold values from -11 to 11
- keys: bfloat16 [8192, 2048], P('seq', 'dp'), may hold values from -6 to 6
- values: bfloat16 [8192, 2048], P('seq', 'dp'), may hold values from -12 to 12
- cotangent: bfloat16 [8192, 2048], P('seq', 'dp'), may hold values from -16 to 16
- out_weight: bfloat16 [2048, 2048], P('seq', 'dp'), may hold values from -0.125 to 0.125
Outputs:
- attended: bfloat16 [8192, 2048], P('seq', 'dp')
- grad_queries: bfloat16 [8192, 2048], P('seq', 'dp')
- grad_keys: bfloat16 [8192, 2048], P('seq', 'dp')
- grad_values: bfloat16 [8192, 2048], P('seq', 'dp')
- grad_out_weight: float32 [2048, 2048], P('seq', 'dp')
The draws below stay inside these ranges and needn't reach their ends.
All inputs are finite; a program needn't handle non-finite values.
Results may differ from the reference program's by a relative error of at most 0.008.
Values may be sent and summed in bfloat16 or wider, within the bound.
No kernel may reach another device: no remote copies, remote signals or barrier semaphores. Data moves between devices by JAX's collectives and lax.ppermute only.
A program may use at most 64 MiB of HBM per device.

```python
import math
import jax
import jax.numpy as jnp
from jax import lax

D = 2048
HEAD = 128
TOK_DEV = 128
HD = 2048
LEN = 8192
LEVELS = 6
N_SEQ = 64


def group_rows(table):
    return jnp.repeat(table, 32, axis=0)


def draw_queries(key, part):
    result = jnp.clip(1.5 * jax.random.normal(jax.random.fold_in(key, 11), (LEN, HD), jnp.float32), -6.0, 6.0)
    return result.astype(jnp.bfloat16)


def draw_keys(key, part):
    fine_rows = jax.random.normal(jax.random.fold_in(key, 12), (LEN, HD), jnp.float32)
    offsets = jax.random.normal(jax.random.fold_in(key, 22), (LEN // 32, HD), jnp.float32)
    result = jnp.clip(fine_rows + group_rows(offsets), -6.0, 6.0)
    return result.astype(jnp.bfloat16)


def draw_values(key, part):
    fine_rows = jax.random.normal(jax.random.fold_in(key, 13), (LEN, HD), jnp.float32)
    offsets = jax.random.normal(jax.random.fold_in(key, 23), (LEN // 32, HD), jnp.float32)
    result = jnp.clip(fine_rows + group_rows(offsets), -8.0, 8.0)
    return result.astype(jnp.bfloat16)


def spiked(entries, own_key, source, target, blocks, factor):
    owner, partner = [(jnp.arange(entries.shape[position]) // (entries.shape[position] // blocks)).reshape([-1 if axis == position else 1 for axis in range(entries.ndim)]) for position in (source, target)]
    chosen = jax.random.permutation(own_key, blocks)[partner]
    strong = (owner == chosen) | (owner == (partner + blocks // 2) % blocks)
    return jnp.where(strong, factor * entries, entries)


def levels(stream_key, shape, cuts, low, top_value):
    def one(position, parts):
        steps = jax.random.uniform(jax.random.fold_in(jax.random.fold_in(stream_key, 6), position), (parts,), jnp.float32, low / len(cuts), top_value / len(cuts))
        return jnp.repeat(jnp.exp(steps), shape[position] // parts).reshape((-1,) + (1,) * (len(shape) - position - 1))

    gain = one(*cuts[0])
    for cut in cuts[1:]:
        gain = gain * one(*cut)
    return gain


def scatter_about(own_key, extent, spread, bound, cuts=(), kind=jnp.bfloat16):
    loudness = levels(own_key, extent, cuts, -0.22, 0.18) if cuts else 1.0
    values = jax.random.normal(own_key, extent, jnp.float32) * spread * loudness
    return jnp.minimum(jnp.maximum(values, -bound), bound).astype(kind)


def heavy_noise(stream_key, shape, width, limit, cuts, heavy, held_as=jnp.bfloat16):
    values = width * jax.random.normal(stream_key, shape, jnp.float32)
    if cuts:
        values = values * levels(stream_key, shape, cuts, -0.22, 0.18)
    return jnp.clip(spiked(values, jax.random.fold_in(stream_key, 3), *heavy), -limit, limit).astype(held_as)


def setup_inputs(seed: int = 0) -> dict:
    streams_of = jax.random.split(jax.random.key(seed), 6)
    queries = draw_queries(jax.random.fold_in(streams_of[5], 71), 0)
    keys = draw_keys(jax.random.fold_in(streams_of[5], 71), 0)
    values = draw_values(jax.random.fold_in(streams_of[5], 71), 0)
    cotangent = heavy_noise(streams_of[3], (LEN, D), 1.0, 16.0, ((0, 64), (1, 8)), (0, 1, 64, 4.0))
    out_weight = scatter_about(streams_of[4], (D, HD), D ** -0.5, 0.125, ((0, 64), (1, 8)))
    return {"queries": queries, "keys": keys, "values": values, "cotangent": cotangent, "out_weight": out_weight}


def sibling_table(table, factor, groups, coarse, layer_bit):
    means = table.reshape(LEN // factor, factor, HD).mean(axis=1)
    swapped = means.reshape(groups // 2, 2, coarse, HD)[:, ::-1].reshape(groups, coarse, HD)
    return jnp.repeat(swapped, 2 ** layer_bit, axis=0)

def return_table(grad_part, factor, groups, coarse, layer_bit):
    summed = grad_part.reshape(groups, 2 ** layer_bit, coarse, HD).sum(axis=1)
    back = summed.reshape(groups // 2, 2, coarse, HD)[:, ::-1].reshape(LEN // factor, HD)
    return jnp.repeat(back / factor, factor, axis=0)

def reference(queries, keys, values, cotangent, out_weight):
    grad_attended = jnp.dot(cotangent, out_weight, preferred_element_type=jnp.float32).astype(jnp.bfloat16)
    blocks = N_SEQ
    tokens = TOK_DEV
    coarse = TOK_DEV // 2
    heads = HD // HEAD
    scale = 1.0 / math.sqrt(HEAD)
    key_float = keys.astype(jnp.float32)
    value_float = values.astype(jnp.float32)
    key_parts = [keys.reshape(blocks, tokens, HD)]
    value_parts = [values.reshape(blocks, tokens, HD)]
    for layer_bit in range(LEVELS):
        factor = 2 ** (layer_bit + 1)
        groups = blocks >> layer_bit
        key_parts.append(sibling_table(key_float, factor, groups, coarse, layer_bit).astype(jnp.bfloat16))
        value_parts.append(sibling_table(value_float, factor, groups, coarse, layer_bit).astype(jnp.bfloat16))
    key_set = jnp.concatenate(key_parts, axis=1)
    value_set = jnp.concatenate(value_parts, axis=1)
    query_blocks = queries.reshape(blocks, tokens, HD)
    grad_blocks = grad_attended.reshape(blocks, tokens, HD)

    def one_head(head_index):
        first = (head_index * HEAD).astype(jnp.int32)
        query_head = lax.dynamic_slice_in_dim(query_blocks, first, HEAD, 2).astype(jnp.float32)
        key_head = lax.dynamic_slice_in_dim(key_set, first, HEAD, 2).astype(jnp.float32)
        value_head = lax.dynamic_slice_in_dim(value_set, first, HEAD, 2).astype(jnp.float32)
        grad_head = lax.dynamic_slice_in_dim(grad_blocks, first, HEAD, 2).astype(jnp.float32)
        scores = jnp.einsum('bta,bka->btk', query_head, key_head) * scale
        peak = lax.optimization_barrier(jnp.max(scores, axis=-1, keepdims=True))
        expo = jnp.exp(scores - peak)
        prob = expo / lax.optimization_barrier(jnp.sum(expo, axis=-1, keepdims=True))
        weights = prob.astype(jnp.bfloat16).astype(jnp.float32)
        attended = jnp.einsum('btk,bka->bta', weights, value_head).astype(jnp.bfloat16)
        grad_weights = jnp.einsum('bta,bka->btk', grad_head, value_head)
        delta = lax.optimization_barrier(jnp.sum(prob * grad_weights, axis=-1, keepdims=True))
        grad_scores = (prob * (grad_weights - delta) * scale).astype(jnp.bfloat16).astype(jnp.float32)
        grad_queries = jnp.einsum('btk,bka->bta', grad_scores, key_head).astype(jnp.bfloat16)
        grad_keyset = jnp.einsum('btk,bta->bka', grad_scores, query_head)
        grad_valset = jnp.einsum('btk,bta->bka', weights, grad_head)
        return (attended, grad_queries, grad_keyset, grad_valset)
    attended, grad_queries, grad_keyset, grad_valset = lax.map(one_head, jnp.arange(heads, dtype=jnp.int32))
    attended = attended.transpose(1, 2, 0, 3).reshape(LEN, HD)
    grad_queries = grad_queries.transpose(1, 2, 0, 3).reshape(LEN, HD)
    grad_keyset = grad_keyset.transpose(1, 2, 0, 3).reshape(blocks, -1, HD)
    grad_valset = grad_valset.transpose(1, 2, 0, 3).reshape(blocks, -1, HD)
    key_total = grad_keyset[:, :tokens].reshape(LEN, HD)
    value_total = grad_valset[:, :tokens].reshape(LEN, HD)
    for layer_bit in range(LEVELS):
        factor = 2 ** (layer_bit + 1)
        groups = blocks >> layer_bit
        first = tokens + layer_bit * coarse
        key_total = key_total + return_table(grad_keyset[:, first:first + coarse], factor, groups, coarse, layer_bit)
        value_total = value_total + return_table(grad_valset[:, first:first + coarse], factor, groups, coarse, layer_bit)
    grad_out_weight = jnp.dot(cotangent.T, attended, preferred_element_type=jnp.float32)
    return (attended, grad_queries, key_total.astype(jnp.bfloat16), value_total.astype(jnp.bfloat16), grad_out_weight)
```

```python
import math

import jax
import jax.numpy as jnp
from jax import lax
from jax.sharding import Mesh
from jax.sharding import PartitionSpec as P

HEAD = 128
SEQ = ("seq_0", "seq_1")
MINOR = "seq_1"


def top_bit(d):
    total = jnp.zeros_like(d) - 1
    for k in range(0, 7):
        total = total + (d >= (1 << k)).astype(d.dtype)
    return total


def pooled(table, factor):
    return table.reshape(table.shape[0], table.shape[1] // factor, factor, table.shape[2]).mean(axis=2)


def pad_rows(x, rows):
    return jnp.pad(x, ((0, 0), (0, rows - x.shape[1]), (0, 0)))


def pick_level(level_of, tables, lo):
    out = tables[-1]
    for i in range(len(tables) - 2, -1, -1):
        mask = (level_of == lo + i).reshape((-1,) + (1,) * (tables[i].ndim - 1))
        out = jnp.where(mask, tables[i], out)
    return out


def sibling_rows(recv, start, level, rows):
    count = 1 << level
    part = lax.dynamic_slice_in_dim(recv, start, count, axis=0)[:, :, :rows]
    part = jnp.moveaxis(part, 0, 1)
    return part.reshape(part.shape[0], count * rows, part.shape[3])


def on_device(queries, keys, values, cotangent, out_weight):
    tokens = queries.shape[0]
    width = queries.shape[1]
    heads = width // HEAD
    coarse = tokens // 2
    scale = 1.0 / math.sqrt(HEAD)
    n_minor = lax.axis_size(MINOR)
    n_seq = lax.axis_size(SEQ)
    depth = n_seq.bit_length() - 1
    minor_depth = n_minor.bit_length() - 1
    position = lax.axis_index(SEQ)
    minor_pos = lax.axis_index(MINOR)
    table = jnp.stack([keys, values]).astype(jnp.float32)
    means = [pooled(table, 2 << m).astype(jnp.bfloat16) for m in range(depth)]

    peers = jnp.arange(n_minor, dtype=jnp.int32)
    near_level = top_bit(minor_pos ^ peers)
    near_send = pick_level(
        near_level,
        [jnp.broadcast_to(pad_rows(means[m], coarse)[None], (n_minor, 2, coarse, width)) for m in range(minor_depth)],
        0,
    )
    near_recv = lax.all_to_all(near_send, MINOR, 0, 0, tiled=True)

    far_rows = coarse >> minor_depth
    w_rows = out_weight.shape[0]
    everyone = jnp.arange(n_seq, dtype=jnp.int32)
    far_level = top_bit(position ^ everyone)
    far_kv = pick_level(
        far_level,
        [jnp.broadcast_to(pad_rows(means[m], far_rows)[None], (n_seq, 2, far_rows, width)) for m in range(minor_depth, depth)],
        minor_depth,
    )
    far_send = jnp.concatenate(
        [jnp.broadcast_to(out_weight[None], (n_seq, w_rows, width)), far_kv.reshape(n_seq, 2 * far_rows, width)], axis=1
    )
    far_recv = lax.all_to_all(far_send, SEQ, 0, 0, tiled=True)
    full_weight = far_recv[:, :w_rows].reshape(n_seq * w_rows, width)
    far_kv_recv = far_recv[:, w_rows:].reshape(n_seq, 2, far_rows, width)

    levels_kv = []
    for m in range(depth):
        start = ((position >> m) ^ 1) << m
        if m < minor_depth:
            levels_kv.append(sibling_rows(near_recv, start & (n_minor - 1), m, coarse >> m))
        else:
            levels_kv.append(sibling_rows(far_kv_recv, start, m, coarse >> m))
    key_set = jnp.concatenate([keys] + [lv[0] for lv in levels_kv], axis=0)
    value_set = jnp.concatenate([values] + [lv[1] for lv in levels_kv], axis=0)

    full_cot = lax.all_to_all(
        jnp.broadcast_to(cotangent[None], (lax.axis_size("dp"),) + cotangent.shape), "dp", 0, 0, tiled=True
    )
    full_cot = jnp.moveaxis(full_cot, 0, 1).reshape(tokens, -1)
    grad_attended = jnp.dot(full_cot, full_weight, preferred_element_type=jnp.float32).astype(jnp.bfloat16)

    attended_parts = []
    grad_query_parts = []
    grad_key_parts = []
    grad_value_parts = []
    for head in range(heads):
        low = head * HEAD
        high = low + HEAD
        query_head = queries[:, low:high]
        key_head = key_set[:, low:high]
        value_head = value_set[:, low:high]
        grad_head = grad_attended[:, low:high]
        scores = (
            jnp.einsum("ta,ka->tk", query_head, key_head, preferred_element_type=jnp.float32)
            * scale
        )
        peak = jnp.max(scores, axis=-1, keepdims=True)
        expo = jnp.exp(scores - peak)
        prob = expo / jnp.sum(expo, axis=-1, keepdims=True)
        weights = prob.astype(jnp.bfloat16)
        attended_parts.append(
            jnp.dot(weights, value_head, preferred_element_type=jnp.float32).astype(jnp.bfloat16)
        )
        grad_weights = jnp.einsum(
            "ta,ka->tk", grad_head, value_head, preferred_element_type=jnp.float32
        )
        delta = jnp.sum(prob * grad_weights, axis=-1, keepdims=True)
        grad_scores = (prob * (grad_weights - delta) * scale).astype(jnp.bfloat16)
        grad_query_parts.append(
            jnp.dot(grad_scores, key_head, preferred_element_type=jnp.float32).astype(jnp.bfloat16)
        )
        grad_key_parts.append(
            jnp.einsum("tk,ta->ka", grad_scores, query_head, preferred_element_type=jnp.float32)
        )
        grad_value_parts.append(
            jnp.einsum("tk,ta->ka", weights, grad_head, preferred_element_type=jnp.float32)
        )
    attended = jnp.concatenate(attended_parts, axis=1)
    grad_queries = jnp.concatenate(grad_query_parts, axis=1)

    grad_out_weight = lax.dot_general(
        full_cot, attended, (((0,), (0,)), ((), ())), preferred_element_type=jnp.float32
    )
    for axis in SEQ:
        grad_out_weight = lax.psum_scatter(grad_out_weight, axis, scatter_dimension=0, tiled=True)

    grad_sets = jnp.stack(
        [jnp.concatenate(grad_key_parts, axis=1), jnp.concatenate(grad_value_parts, axis=1)]
    )
    level_grads = []
    for m in range(depth):
        first = tokens + m * coarse
        part = grad_sets[:, first : first + coarse].astype(jnp.bfloat16)
        level_grads.append(part.reshape(2, 1 << m, coarse >> m, width))

    near_back = pick_level(
        near_level,
        [
            jnp.stack([pad_rows(level_grads[m][:, k & ((1 << m) - 1)], coarse) for k in range(n_minor)])
            for m in range(minor_depth)
        ],
        0,
    )
    near_got = lax.all_to_all(near_back, MINOR, 0, 0, tiled=True).astype(jnp.float32)
    far_back = pick_level(
        far_level,
        [
            jnp.stack([pad_rows(level_grads[m][:, c & ((1 << m) - 1)], far_rows) for c in range(n_seq)])
            for m in range(minor_depth, depth)
        ],
        minor_depth,
    )
    far_got = lax.all_to_all(far_back, SEQ, 0, 0, tiled=True).astype(jnp.float32)

    own_grads = grad_sets[:, :tokens]
    for m in range(depth):
        rows = coarse >> m
        if m < minor_depth:
            got, level_of = near_got, near_level
        else:
            got, level_of = far_got, far_level
        mask = (level_of == m).reshape(-1, 1, 1, 1)
        summed = jnp.sum(jnp.where(mask, got[:, :, :rows], 0.0), axis=0)
        factor = 2 << m
        spread = jnp.broadcast_to((summed / factor)[:, :, None], (2, rows, factor, width))
        own_grads = own_grads + spread.reshape(2, tokens, width)
    grad_keys = own_grads[0].astype(jnp.bfloat16)
    grad_values = own_grads[1].astype(jnp.bfloat16)
    return (attended, grad_queries, grad_keys, grad_values, grad_out_weight)


def solution(mesh):
    n_seq = mesh.shape["seq"]
    minor = 1 << ((n_seq.bit_length() - 1 + 1) // 2)
    torus = Mesh(mesh.devices.reshape(n_seq // minor, minor, mesh.shape["dp"]), ("seq_0", "seq_1", "dp"))
    placed = (P(SEQ, "dp"),) * 5
    return jax.shard_map(
        on_device,
        mesh=torus,
        in_specs=placed,
        out_specs=(P(SEQ, "dp"),) * 5,
        check_vma=False,
    )
```

```python
import math

import jax
import jax.numpy as jnp
from jax import lax
from jax.sharding import Mesh
from jax.sharding import PartitionSpec as P

HEAD = 128
SEQ = ("seq_0", "seq_1")


def from_partner(block, axis, apart):
    count = lax.axis_size(axis)
    route = []
    for low in range(count):
        high = low | 1 << apart
        if high != low and high < count:
            route += [(low, high), (high, low)]
    return lax.ppermute(block, axis, route)


def joined_along(blocks, dim):
    blocks = jnp.moveaxis(blocks, 0, dim)
    dims = blocks.shape
    return blocks.reshape(*dims[:dim], dims[dim] * dims[dim + 1], *dims[dim + 2 :])


def from_everyone(x, axis):
    copies = jnp.broadcast_to(x, (lax.axis_size(axis), *x.shape))
    return lax.all_to_all(copies, axis, split_axis=0, concat_axis=0, tiled=True)


def gathered_copies(x, axis, dim):
    return joined_along(from_everyone(x, axis), dim)


def own_rows(running, axes):
    first, last = axes
    running = lax.psum_scatter(running, first, scatter_dimension=0, tiled=True)
    count = lax.axis_size(last)
    parts = running.reshape(count, running.shape[0] // count, running.shape[1])
    return jnp.sum(lax.all_to_all(parts, last, 0, 0, tiled=True), axis=0)


def pair_mean(table):
    paired = table.reshape(table.shape[0], table.shape[1] // 2, 2, table.shape[2])
    return (paired[:, :, 0] + paired[:, :, 1]) * 0.5


def spread_rows(table):
    doubled = jnp.broadcast_to(
        table[:, :, None], (table.shape[0], table.shape[1], 2, table.shape[2])
    )
    return doubled.reshape(table.shape[0], table.shape[1] * 2, table.shape[2])


def on_device(queries, keys, values, cotangent, out_weight):
    tokens = queries.shape[0]
    width = queries.shape[1]
    heads = width // HEAD
    coarse = tokens // 2
    scale = 1.0 / math.sqrt(HEAD)
    depth = lax.axis_size(SEQ).bit_length() - 1
    position = lax.axis_index(SEQ)
    own_table = pair_mean(jnp.stack([keys, values]).astype(jnp.float32))
    far_keys = []
    far_values = []
    for layer_bit in range(depth):
        far_table = from_partner(own_table, SEQ, layer_bit)
        far_keys.append(far_table[0].astype(jnp.bfloat16))
        far_values.append(far_table[1].astype(jnp.bfloat16))
        if layer_bit + 1 < depth:
            lower_half = position >> layer_bit & 1 == 0
            joined = jnp.concatenate(
                [
                    jnp.where(lower_half, own_table, far_table),
                    jnp.where(lower_half, far_table, own_table),
                ],
                axis=1,
            )
            own_table = pair_mean(joined)
    key_set = jnp.concatenate([keys] + far_keys, axis=0)
    value_set = jnp.concatenate([values] + far_values, axis=0)
    full_cot = gathered_copies(cotangent, "dp", 1)
    full_weight = gathered_copies(out_weight, SEQ, 0)
    grad_attended = jnp.dot(full_cot, full_weight, preferred_element_type=jnp.float32).astype(
        jnp.bfloat16
    )
    attended_parts = []
    grad_query_parts = []
    grad_key_parts = []
    grad_value_parts = []
    for head in range(heads):
        low = head * HEAD
        high = low + HEAD
        query_head = queries[:, low:high]
        key_head = key_set[:, low:high]
        value_head = value_set[:, low:high]
        grad_head = grad_attended[:, low:high]
        scores = (
            jnp.einsum("ta,ka->tk", query_head, key_head, preferred_element_type=jnp.float32)
            * scale
        )
        peak = jnp.max(scores, axis=-1, keepdims=True)
        expo = jnp.exp(scores - peak)
        prob = expo / jnp.sum(expo, axis=-1, keepdims=True)
        weights = prob.astype(jnp.bfloat16)
        attended_parts.append(
            jnp.dot(weights, value_head, preferred_element_type=jnp.float32).astype(jnp.bfloat16)
        )
        grad_weights = jnp.einsum(
            "ta,ka->tk", grad_head, value_head, preferred_element_type=jnp.float32
        )
        delta = jnp.sum(prob * grad_weights, axis=-1, keepdims=True)
        grad_scores = (prob * (grad_weights - delta) * scale).astype(jnp.bfloat16)
        grad_query_parts.append(
            jnp.dot(grad_scores, key_head, preferred_element_type=jnp.float32).astype(jnp.bfloat16)
        )
        grad_key_parts.append(
            jnp.einsum("tk,ta->ka", grad_scores, query_head, preferred_element_type=jnp.float32)
        )
        grad_value_parts.append(
            jnp.einsum("tk,ta->ka", weights, grad_head, preferred_element_type=jnp.float32)
        )
    attended = jnp.concatenate(attended_parts, axis=1)
    grad_queries = jnp.concatenate(grad_query_parts, axis=1)
    grad_sets = jnp.stack(
        [jnp.concatenate(grad_key_parts, axis=1), jnp.concatenate(grad_value_parts, axis=1)]
    )
    carried = jnp.zeros((2, coarse, width), jnp.float32)
    for layer_bit in reversed(range(depth)):
        first = tokens + layer_bit * coarse
        outgoing = grad_sets[:, first : first + coarse]
        kept = jnp.zeros((2, coarse, width), jnp.float32)
        if layer_bit + 1 < depth:
            lower_half = position >> layer_bit & 1 == 0
            spread = spread_rows(carried * 0.5)
            low_part = spread[:, :coarse]
            high_part = spread[:, coarse:]
            kept = jnp.where(lower_half, low_part, high_part)
            outgoing = outgoing + jnp.where(lower_half, high_part, low_part)
        incoming = from_partner(outgoing.astype(jnp.bfloat16), SEQ, layer_bit).astype(
            outgoing.dtype
        )
        carried = kept + incoming
    own_grads = grad_sets[:, :tokens] + spread_rows(carried * 0.5)
    grad_keys = own_grads[0].astype(jnp.bfloat16)
    grad_values = own_grads[1].astype(jnp.bfloat16)
    grad_out_weight = own_rows(
        lax.dot_general(
            full_cot, attended, (((0,), (0,)), ((), ())), preferred_element_type=jnp.float32
        ),
        SEQ,
    )
    return (attended, grad_queries, grad_keys, grad_values, grad_out_weight)


def solution(mesh):
    torus = Mesh(mesh.devices.reshape(8, 8, mesh.shape["dp"]), ("seq_0", "seq_1", "dp"))
    placed = (P(SEQ, "dp"), P(SEQ, "dp"), P(SEQ, "dp"), P(SEQ, "dp"), P(SEQ, "dp"))
    return jax.shard_map(
        on_device,
        mesh=torus,
        in_specs=placed,
        out_specs=(P(SEQ, "dp"), P(SEQ, "dp"), P(SEQ, "dp"), P(SEQ, "dp"), P(SEQ, "dp")),
        check_vma=False,
    )
```

```python
import math

import jax
import jax.numpy as jnp
from jax import lax
from jax.sharding import Mesh
from jax.sharding import PartitionSpec as P

HEAD = 128
SEQ = ("seq_0", "seq_1")


def from_partner(block, axis, apart):
    count = lax.axis_size(axis)
    route = []
    for low in range(count):
        high = low | 1 << apart
        if high != low and high < count:
            route += [(low, high), (high, low)]
    return lax.ppermute(block, axis, route)


def joined_along(blocks, dim):
    blocks = jnp.moveaxis(blocks, 0, dim)
    dims = blocks.shape
    return blocks.reshape(*dims[:dim], dims[dim] * dims[dim + 1], *dims[dim + 2 :])


def from_everyone(x, axis):
    copies = jnp.broadcast_to(x, (lax.axis_size(axis), *x.shape))
    return lax.all_to_all(copies, axis, split_axis=0, concat_axis=0, tiled=True)


def gathered_copies(x, axis, dim):
    return joined_along(from_everyone(x, axis), dim)


def own_rows(running, axes):
    first, last = axes
    running = lax.psum_scatter(running, first, scatter_dimension=0, tiled=True)
    count = lax.axis_size(last)
    parts = running.reshape(count, running.shape[0] // count, running.shape[1])
    return jnp.sum(lax.all_to_all(parts, last, 0, 0, tiled=True), axis=0)


def pair_mean(table):
    paired = table.reshape(table.shape[0], table.shape[1] // 2, 2, table.shape[2])
    return (paired[:, :, 0] + paired[:, :, 1]) * 0.5


def spread_rows(table):
    doubled = jnp.broadcast_to(
        table[:, :, None], (table.shape[0], table.shape[1], 2, table.shape[2])
    )
    return doubled.reshape(table.shape[0], table.shape[1] * 2, table.shape[2])


def top_bit(d):
    total = jnp.zeros_like(d) - 1
    for k in range(0, 7):
        total = total + (d >= (1 << k)).astype(d.dtype)
    return total


def pooled(table, factor):
    return table.reshape(table.shape[0], table.shape[1] // factor, factor, table.shape[2]).mean(axis=2)


def pad_rows(x, rows):
    return jnp.pad(x, ((0, 0), (0, rows - x.shape[1]), (0, 0)))


def pick_level(level_of, tables, lo):
    out = tables[-1]
    for i in range(len(tables) - 2, -1, -1):
        mask = (level_of == lo + i).reshape((-1,) + (1,) * (tables[i].ndim - 1))
        out = jnp.where(mask, tables[i], out)
    return out


def sibling_rows(recv, start, level, rows):
    count = 1 << level
    part = lax.dynamic_slice_in_dim(recv, start, count, axis=0)[:, :, :rows]
    part = jnp.moveaxis(part, 0, 1)
    return part.reshape(part.shape[0], count * rows, part.shape[3])


def swap_major(block, axis, bit):
    count = lax.axis_size(axis)
    return lax.ppermute(block, axis, [(i, i ^ (1 << bit)) for i in range(count)])


def on_device(queries, keys, values, cotangent, out_weight):
    tokens = queries.shape[0]
    width = queries.shape[1]
    heads = width // HEAD
    coarse = tokens // 2
    scale = 1.0 / math.sqrt(HEAD)
    depth = lax.axis_size(SEQ).bit_length() - 1
    position = lax.axis_index(SEQ)
    major, minor = SEQ
    n_minor = lax.axis_size(minor)
    minor_depth = n_minor.bit_length() - 1
    minor_pos = lax.axis_index(minor)
    major_pos = lax.axis_index(major)
    table = jnp.stack([keys, values]).astype(jnp.float32)
    means = [pooled(table, 2 << m).astype(jnp.bfloat16) for m in range(depth)]
    peers = jnp.arange(n_minor, dtype=jnp.int32)
    near_level = top_bit(minor_pos ^ peers)
    near_kv = pick_level(
        near_level,
        [jnp.broadcast_to(pad_rows(means[m], coarse)[None], (n_minor, 2, coarse, width)) for m in range(minor_depth)],
        0,
    )
    upper = jnp.concatenate(means[minor_depth:], axis=1)
    near_send = jnp.concatenate(
        [near_kv, jnp.broadcast_to(upper[None], (n_minor,) + upper.shape)], axis=2
    )
    near_recv = lax.all_to_all(near_send, minor, 0, 0, tiled=True)
    levels_kv = []
    for m in range(minor_depth):
        start = ((minor_pos >> m) ^ 1) << m
        levels_kv.append(sibling_rows(near_recv[:, :, :coarse], start, m, coarse >> m))
    slices = []
    offset = coarse
    for m in range(minor_depth, depth):
        rows = coarse >> m
        part = jnp.moveaxis(near_recv[:, :, offset : offset + rows], 0, 1)
        slices.append(part.reshape(2, n_minor * rows, width))
        offset += rows
    for r in range(depth - minor_depth):
        got = swap_major(jnp.concatenate(slices, axis=1), major, r)
        levels_kv.append(got[:, :coarse])
        lower_half = (major_pos >> r) & 1 == 0
        joined = []
        used = coarse
        for own in slices[1:]:
            far = got[:, used : used + own.shape[1]]
            used += own.shape[1]
            joined.append(
                jnp.where(lower_half, jnp.concatenate([own, far], 1), jnp.concatenate([far, own], 1))
            )
        slices = joined
    key_set = jnp.concatenate([keys] + [lv[0] for lv in levels_kv], axis=0)
    value_set = jnp.concatenate([values] + [lv[1] for lv in levels_kv], axis=0)
    full_cot = gathered_copies(cotangent, "dp", 1)
    full_weight = gathered_copies(out_weight, SEQ, 0)
    grad_attended = jnp.dot(full_cot, full_weight, preferred_element_type=jnp.float32).astype(
        jnp.bfloat16
    )
    attended_parts = []
    grad_query_parts = []
    grad_key_parts = []
    grad_value_parts = []
    for head in range(heads):
        low = head * HEAD
        high = low + HEAD
        query_head = queries[:, low:high]
        key_head = key_set[:, low:high]
        value_head = value_set[:, low:high]
        grad_head = grad_attended[:, low:high]
        scores = (
            jnp.einsum("ta,ka->tk", query_head, key_head, preferred_element_type=jnp.float32)
            * scale
        )
        peak = jnp.max(scores, axis=-1, keepdims=True)
        expo = jnp.exp(scores - peak)
        prob = expo / jnp.sum(expo, axis=-1, keepdims=True)
        weights = prob.astype(jnp.bfloat16)
        attended_parts.append(
            jnp.dot(weights, value_head, preferred_element_type=jnp.float32).astype(jnp.bfloat16)
        )
        grad_weights = jnp.einsum(
            "ta,ka->tk", grad_head, value_head, preferred_element_type=jnp.float32
        )
        delta = jnp.sum(prob * grad_weights, axis=-1, keepdims=True)
        grad_scores = (prob * (grad_weights - delta) * scale).astype(jnp.bfloat16)
        grad_query_parts.append(
            jnp.dot(grad_scores, key_head, preferred_element_type=jnp.float32).astype(jnp.bfloat16)
        )
        grad_key_parts.append(
            jnp.einsum("tk,ta->ka", grad_scores, query_head, preferred_element_type=jnp.float32)
        )
        grad_value_parts.append(
            jnp.einsum("tk,ta->ka", weights, grad_head, preferred_element_type=jnp.float32)
        )
    attended = jnp.concatenate(attended_parts, axis=1)
    grad_queries = jnp.concatenate(grad_query_parts, axis=1)
    grad_sets = jnp.stack(
        [jnp.concatenate(grad_key_parts, axis=1), jnp.concatenate(grad_value_parts, axis=1)]
    )
    carried = jnp.zeros((2, coarse, width), jnp.float32)
    for layer_bit in reversed(range(depth)):
        first = tokens + layer_bit * coarse
        outgoing = grad_sets[:, first : first + coarse]
        kept = jnp.zeros((2, coarse, width), jnp.float32)
        if layer_bit + 1 < depth:
            lower_half = position >> layer_bit & 1 == 0
            spread = spread_rows(carried * 0.5)
            low_part = spread[:, :coarse]
            high_part = spread[:, coarse:]
            kept = jnp.where(lower_half, low_part, high_part)
            outgoing = outgoing + jnp.where(lower_half, high_part, low_part)
        incoming = from_partner(outgoing.astype(jnp.bfloat16), SEQ, layer_bit).astype(
            outgoing.dtype
        )
        carried = kept + incoming
    own_grads = grad_sets[:, :tokens] + spread_rows(carried * 0.5)
    grad_keys = own_grads[0].astype(jnp.bfloat16)
    grad_values = own_grads[1].astype(jnp.bfloat16)
    grad_out_weight = own_rows(
        lax.dot_general(
            full_cot, attended, (((0,), (0,)), ((), ())), preferred_element_type=jnp.float32
        ),
        SEQ,
    )
    return (attended, grad_queries, grad_keys, grad_values, grad_out_weight)


def solution(mesh):
    torus = Mesh(mesh.devices.reshape(8, 8, mesh.shape["dp"]), ("seq_0", "seq_1", "dp"))
    placed = (P(SEQ, "dp"), P(SEQ, "dp"), P(SEQ, "dp"), P(SEQ, "dp"), P(SEQ, "dp"))
    return jax.shard_map(
        on_device,
        mesh=torus,
        in_specs=placed,
        out_specs=(P(SEQ, "dp"), P(SEQ, "dp"), P(SEQ, "dp"), P(SEQ, "dp"), P(SEQ, "dp")),
        check_vma=False,
    )
```

```python
import math

import jax
import jax.numpy as jnp
from jax import lax
from jax.sharding import Mesh
from jax.sharding import PartitionSpec as P

HEAD = 128
SEQ = ("seq_0", "seq_1")


def from_partner(block, axis, apart):
    count = lax.axis_size(axis)
    route = []
    for low in range(count):
        high = low | 1 << apart
        if high != low and high < count:
            route += [(low, high), (high, low)]
    return lax.ppermute(block, axis, route)


def joined_along(blocks, dim):
    blocks = jnp.moveaxis(blocks, 0, dim)
    dims = blocks.shape
    return blocks.reshape(*dims[:dim], dims[dim] * dims[dim + 1], *dims[dim + 2 :])


def from_everyone(x, axis):
    copies = jnp.broadcast_to(x, (lax.axis_size(axis), *x.shape))
    return lax.all_to_all(copies, axis, split_axis=0, concat_axis=0, tiled=True)


def gathered_copies(x, axis, dim):
    return joined_along(from_everyone(x, axis), dim)


def own_rows(running, axes):
    first, last = axes
    running = lax.psum_scatter(running, first, scatter_dimension=0, tiled=True)
    count = lax.axis_size(last)
    parts = running.reshape(count, running.shape[0] // count, running.shape[1])
    return jnp.sum(lax.all_to_all(parts, last, 0, 0, tiled=True), axis=0)


def pair_mean(table):
    paired = table.reshape(table.shape[0], table.shape[1] // 2, 2, table.shape[2])
    return (paired[:, :, 0] + paired[:, :, 1]) * 0.5


def spread_rows(table):
    doubled = jnp.broadcast_to(
        table[:, :, None], (table.shape[0], table.shape[1], 2, table.shape[2])
    )
    return doubled.reshape(table.shape[0], table.shape[1] * 2, table.shape[2])


def top_bit(d):
    total = jnp.zeros_like(d) - 1
    for k in range(0, 7):
        total = total + (d >= (1 << k)).astype(d.dtype)
    return total


def pooled(table, factor):
    return table.reshape(table.shape[0], table.shape[1] // factor, factor, table.shape[2]).mean(axis=2)


def pad_rows(x, rows):
    return jnp.pad(x, ((0, 0), (0, rows - x.shape[1]), (0, 0)))


def pick_level(level_of, tables, lo):
    out = tables[-1]
    for i in range(len(tables) - 2, -1, -1):
        mask = (level_of == lo + i).reshape((-1,) + (1,) * (tables[i].ndim - 1))
        out = jnp.where(mask, tables[i], out)
    return out


def sibling_rows(recv, start, level, rows):
    count = 1 << level
    part = lax.dynamic_slice_in_dim(recv, start, count, axis=0)[:, :, :rows]
    part = jnp.moveaxis(part, 0, 1)
    return part.reshape(part.shape[0], count * rows, part.shape[3])


def swap_major(block, axis, bit):
    count = lax.axis_size(axis)
    return lax.ppermute(block, axis, [(i, i ^ (1 << bit)) for i in range(count)])


def on_device(queries, keys, values, cotangent, out_weight):
    tokens = queries.shape[0]
    width = queries.shape[1]
    heads = width // HEAD
    coarse = tokens // 2
    scale = 1.0 / math.sqrt(HEAD)
    depth = lax.axis_size(SEQ).bit_length() - 1
    position = lax.axis_index(SEQ)
    major, minor = SEQ
    n_minor = lax.axis_size(minor)
    minor_depth = n_minor.bit_length() - 1
    minor_pos = lax.axis_index(minor)
    major_pos = lax.axis_index(major)
    table = jnp.stack([keys, values]).astype(jnp.float32)
    means = []
    running = table
    for m in range(depth):
        running = pair_mean(running)
        means.append(running.astype(jnp.bfloat16))
    peers = jnp.arange(n_minor, dtype=jnp.int32)
    near_level = top_bit(minor_pos ^ peers)
    near_kv = pick_level(
        near_level,
        [jnp.broadcast_to(pad_rows(means[m], coarse)[None], (n_minor, 2, coarse, width)) for m in range(minor_depth)],
        0,
    )
    upper = jnp.concatenate(means[minor_depth:], axis=1)
    near_send = jnp.concatenate(
        [near_kv, jnp.broadcast_to(upper[None], (n_minor,) + upper.shape)], axis=2
    )
    kv_rows = near_send.shape[2]
    w_rows = out_weight.shape[0]
    near_send = jnp.concatenate(
        [near_send.reshape(n_minor, 2 * kv_rows, width), jnp.broadcast_to(out_weight[None], (n_minor, w_rows, width))],
        axis=1,
    )
    near_all = lax.all_to_all(near_send, minor, 0, 0, tiled=True)
    near_recv = near_all[:, : 2 * kv_rows].reshape(n_minor, 2, kv_rows, width)
    weight_rows = near_all[:, 2 * kv_rows :].reshape(n_minor * w_rows, width)
    levels_kv = []
    for m in range(minor_depth):
        start = ((minor_pos >> m) ^ 1) << m
        levels_kv.append(sibling_rows(near_recv[:, :, :coarse], start, m, coarse >> m))
    slices = []
    offset = coarse
    for m in range(minor_depth, depth):
        rows = coarse >> m
        part = jnp.moveaxis(near_recv[:, :, offset : offset + rows], 0, 1)
        slices.append(part.reshape(2, n_minor * rows, width))
        offset += rows
    for r in range(depth - minor_depth):
        kv_all = jnp.concatenate(slices, axis=1)
        kv_count = kv_all.shape[1]
        payload = jnp.concatenate([kv_all.reshape(2 * kv_count, width), weight_rows], axis=0)
        arrived = swap_major(payload, major, r)
        got = arrived[: 2 * kv_count].reshape(2, kv_count, width)
        far_weight = arrived[2 * kv_count :]
        levels_kv.append(got[:, :coarse])
        lower_half = (major_pos >> r) & 1 == 0
        weight_rows = jnp.where(
            lower_half,
            jnp.concatenate([weight_rows, far_weight], 0),
            jnp.concatenate([far_weight, weight_rows], 0),
        )
        joined = []
        used = coarse
        for own in slices[1:]:
            far = got[:, used : used + own.shape[1]]
            used += own.shape[1]
            joined.append(
                jnp.where(lower_half, jnp.concatenate([own, far], 1), jnp.concatenate([far, own], 1))
            )
        slices = joined
    key_set = jnp.concatenate([keys] + [lv[0] for lv in levels_kv], axis=0)
    value_set = jnp.concatenate([values] + [lv[1] for lv in levels_kv], axis=0)
    full_cot = gathered_copies(cotangent, "dp", 1)
    full_weight = weight_rows
    grad_attended = jnp.dot(full_cot, full_weight, preferred_element_type=jnp.float32).astype(
        jnp.bfloat16
    )
    attended_parts = []
    grad_query_parts = []
    grad_key_parts = []
    grad_value_parts = []
    for head in range(heads):
        low = head * HEAD
        high = low + HEAD
        query_head = queries[:, low:high]
        key_head = key_set[:, low:high]
        value_head = value_set[:, low:high]
        grad_head = grad_attended[:, low:high]
        scores = (
            jnp.einsum("ta,ka->tk", query_head, key_head, preferred_element_type=jnp.float32)
            * scale
        )
        peak = jnp.max(scores, axis=-1, keepdims=True)
        expo = jnp.exp(scores - peak)
        prob = expo / jnp.sum(expo, axis=-1, keepdims=True)
        weights = prob.astype(jnp.bfloat16)
        attended_parts.append(
            jnp.dot(weights, value_head, preferred_element_type=jnp.float32).astype(jnp.bfloat16)
        )
        grad_weights = jnp.einsum(
            "ta,ka->tk", grad_head, value_head, preferred_element_type=jnp.float32
        )
        delta = jnp.sum(prob * grad_weights, axis=-1, keepdims=True)
        grad_scores = (prob * (grad_weights - delta) * scale).astype(jnp.bfloat16)
        grad_query_parts.append(
            jnp.dot(grad_scores, key_head, preferred_element_type=jnp.float32).astype(jnp.bfloat16)
        )
        grad_key_parts.append(
            jnp.einsum("tk,ta->ka", grad_scores, query_head, preferred_element_type=jnp.float32)
        )
        grad_value_parts.append(
            jnp.einsum("tk,ta->ka", weights, grad_head, preferred_element_type=jnp.float32)
        )
    attended = jnp.concatenate(attended_parts, axis=1)
    grad_queries = jnp.concatenate(grad_query_parts, axis=1)
    grad_sets = jnp.stack(
        [jnp.concatenate(grad_key_parts, axis=1), jnp.concatenate(grad_value_parts, axis=1)]
    )
    carried = jnp.zeros((2, coarse, width), jnp.float32)
    for layer_bit in reversed(range(depth)):
        first = tokens + layer_bit * coarse
        outgoing = grad_sets[:, first : first + coarse]
        kept = jnp.zeros((2, coarse, width), jnp.float32)
        if layer_bit + 1 < depth:
            lower_half = position >> layer_bit & 1 == 0
            spread = spread_rows(carried * 0.5)
            low_part = spread[:, :coarse]
            high_part = spread[:, coarse:]
            kept = jnp.where(lower_half, low_part, high_part)
            outgoing = outgoing + jnp.where(lower_half, high_part, low_part)
        incoming = from_partner(outgoing.astype(jnp.bfloat16), SEQ, layer_bit).astype(
            outgoing.dtype
        )
        carried = kept + incoming
    own_grads = grad_sets[:, :tokens] + spread_rows(carried * 0.5)
    grad_keys = own_grads[0].astype(jnp.bfloat16)
    grad_values = own_grads[1].astype(jnp.bfloat16)
    grad_out_weight = own_rows(
        lax.dot_general(
            full_cot, attended, (((0,), (0,)), ((), ())), preferred_element_type=jnp.float32
        ),
        SEQ,
    )
    return (attended, grad_queries, grad_keys, grad_values, grad_out_weight)


def solution(mesh):
    torus = Mesh(mesh.devices.reshape(8, 8, mesh.shape["dp"]), ("seq_0", "seq_1", "dp"))
    placed = (P(SEQ, "dp"), P(SEQ, "dp"), P(SEQ, "dp"), P(SEQ, "dp"), P(SEQ, "dp"))
    return jax.shard_map(
        on_device,
        mesh=torus,
        in_specs=placed,
        out_specs=(P(SEQ, "dp"), P(SEQ, "dp"), P(SEQ, "dp"), P(SEQ, "dp"), P(SEQ, "dp")),
        check_vma=False,
    )
```

```python
import math

import jax
import jax.numpy as jnp
from jax import lax
from jax.sharding import Mesh
from jax.sharding import PartitionSpec as P

HEAD = 128
SEQ = ("seq_0", "seq_1")


def from_partner(block, axis, apart):
    count = lax.axis_size(axis)
    route = []
    for low in range(count):
        high = low | 1 << apart
        if high != low and high < count:
            route += [(low, high), (high, low)]
    return lax.ppermute(block, axis, route)


def joined_along(blocks, dim):
    blocks = jnp.moveaxis(blocks, 0, dim)
    dims = blocks.shape
    return blocks.reshape(*dims[:dim], dims[dim] * dims[dim + 1], *dims[dim + 2 :])


def from_everyone(x, axis):
    copies = jnp.broadcast_to(x, (lax.axis_size(axis), *x.shape))
    return lax.all_to_all(copies, axis, split_axis=0, concat_axis=0, tiled=True)


def gathered_copies(x, axis, dim):
    return joined_along(from_everyone(x, axis), dim)


def own_rows(running, axes):
    count = lax.axis_size(axes)
    parts = running.astype(jnp.bfloat16).reshape(count, running.shape[0] // count, running.shape[1])
    return jnp.sum(lax.all_to_all(parts, axes, 0, 0, tiled=True).astype(jnp.float32), axis=0)


def pair_mean(table):
    paired = table.reshape(table.shape[0], table.shape[1] // 2, 2, table.shape[2])
    return (paired[:, :, 0] + paired[:, :, 1]) * 0.5


def spread_rows(table):
    doubled = jnp.broadcast_to(
        table[:, :, None], (table.shape[0], table.shape[1], 2, table.shape[2])
    )
    return doubled.reshape(table.shape[0], table.shape[1] * 2, table.shape[2])


def on_device(queries, keys, values, cotangent, out_weight):
    tokens = queries.shape[0]
    width = queries.shape[1]
    heads = width // HEAD
    coarse = tokens // 2
    scale = 1.0 / math.sqrt(HEAD)
    depth = lax.axis_size(SEQ).bit_length() - 1
    position = lax.axis_index(SEQ)
    own_table = pair_mean(jnp.stack([keys, values]).astype(jnp.float32))
    far_keys = []
    far_values = []
    for layer_bit in range(depth):
        far_table = from_partner(own_table, SEQ, layer_bit)
        far_keys.append(far_table[0].astype(jnp.bfloat16))
        far_values.append(far_table[1].astype(jnp.bfloat16))
        if layer_bit + 1 < depth:
            lower_half = position >> layer_bit & 1 == 0
            joined = jnp.concatenate(
                [
                    jnp.where(lower_half, own_table, far_table),
                    jnp.where(lower_half, far_table, own_table),
                ],
                axis=1,
            )
            own_table = pair_mean(joined)
    key_set = jnp.concatenate([keys] + far_keys, axis=0)
    value_set = jnp.concatenate([values] + far_values, axis=0)
    full_cot = gathered_copies(cotangent, "dp", 1)
    full_weight = gathered_copies(out_weight, SEQ, 0)
    grad_attended = jnp.dot(full_cot, full_weight, preferred_element_type=jnp.float32).astype(
        jnp.bfloat16
    )
    attended_parts = []
    grad_query_parts = []
    grad_key_parts = []
    grad_value_parts = []
    for head in range(heads):
        low = head * HEAD
        high = low + HEAD
        query_head = queries[:, low:high]
        key_head = key_set[:, low:high]
        value_head = value_set[:, low:high]
        grad_head = grad_attended[:, low:high]
        scores = (
            jnp.einsum("ta,ka->tk", query_head, key_head, preferred_element_type=jnp.float32)
            * scale
        )
        peak = jnp.max(scores, axis=-1, keepdims=True)
        expo = jnp.exp(scores - peak)
        prob = expo / jnp.sum(expo, axis=-1, keepdims=True)
        weights = prob.astype(jnp.bfloat16)
        attended_parts.append(
            jnp.dot(weights, value_head, preferred_element_type=jnp.float32).astype(jnp.bfloat16)
        )
        grad_weights = jnp.einsum(
            "ta,ka->tk", grad_head, value_head, preferred_element_type=jnp.float32
        )
        delta = jnp.sum(prob * grad_weights, axis=-1, keepdims=True)
        grad_scores = (prob * (grad_weights - delta) * scale).astype(jnp.bfloat16)
        grad_query_parts.append(
            jnp.dot(grad_scores, key_head, preferred_element_type=jnp.float32).astype(jnp.bfloat16)
        )
        grad_key_parts.append(
            jnp.einsum("tk,ta->ka", grad_scores, query_head, preferred_element_type=jnp.float32)
        )
        grad_value_parts.append(
            jnp.einsum("tk,ta->ka", weights, grad_head, preferred_element_type=jnp.float32)
        )
    attended = jnp.concatenate(attended_parts, axis=1)
    grad_queries = jnp.concatenate(grad_query_parts, axis=1)
    grad_sets = jnp.stack(
        [jnp.concatenate(grad_key_parts, axis=1), jnp.concatenate(grad_value_parts, axis=1)]
    )
    carried = jnp.zeros((2, coarse, width), jnp.float32)
    for layer_bit in reversed(range(depth)):
        first = tokens + layer_bit * coarse
        outgoing = grad_sets[:, first : first + coarse]
        kept = jnp.zeros((2, coarse, width), jnp.float32)
        if layer_bit + 1 < depth:
            lower_half = position >> layer_bit & 1 == 0
            spread = spread_rows(carried * 0.5)
            low_part = spread[:, :coarse]
            high_part = spread[:, coarse:]
            kept = jnp.where(lower_half, low_part, high_part)
            outgoing = outgoing + jnp.where(lower_half, high_part, low_part)
        incoming = from_partner(outgoing.astype(jnp.bfloat16), SEQ, layer_bit).astype(
            outgoing.dtype
        )
        carried = kept + incoming
    own_grads = grad_sets[:, :tokens] + spread_rows(carried * 0.5)
    grad_keys = own_grads[0].astype(jnp.bfloat16)
    grad_values = own_grads[1].astype(jnp.bfloat16)
    grad_out_weight = own_rows(
        lax.dot_general(
            full_cot, attended, (((0,), (0,)), ((), ())), preferred_element_type=jnp.float32
        ),
        SEQ,
    )
    return (attended, grad_queries, grad_keys, grad_values, grad_out_weight)


def solution(mesh):
    torus = Mesh(mesh.devices.reshape(8, 8, mesh.shape["dp"]), ("seq_0", "seq_1", "dp"))
    placed = (P(SEQ, "dp"), P(SEQ, "dp"), P(SEQ, "dp"), P(SEQ, "dp"), P(SEQ, "dp"))
    return jax.shard_map(
        on_device,
        mesh=torus,
        in_specs=placed,
        out_specs=(P(SEQ, "dp"), P(SEQ, "dp"), P(SEQ, "dp"), P(SEQ, "dp"), P(SEQ, "dp")),
        check_vma=False,
    )
```

```python
import math

import jax
import jax.numpy as jnp
from jax import lax
from jax.sharding import Mesh
from jax.sharding import PartitionSpec as P

HEAD = 128
SEQ = ("seq_0", "seq_1")


def from_partner(block, axis, apart):
    count = lax.axis_size(axis)
    route = []
    for low in range(count):
        high = low | 1 << apart
        if high != low and high < count:
            route += [(low, high), (high, low)]
    return lax.ppermute(block, axis, route)


def joined_along(blocks, dim):
    blocks = jnp.moveaxis(blocks, 0, dim)
    dims = blocks.shape
    return blocks.reshape(*dims[:dim], dims[dim] * dims[dim + 1], *dims[dim + 2 :])


def from_everyone(x, axis):
    copies = jnp.broadcast_to(x, (lax.axis_size(axis), *x.shape))
    return lax.all_to_all(copies, axis, split_axis=0, concat_axis=0, tiled=True)


def gathered_copies(x, axis, dim):
    return joined_along(from_everyone(x, axis), dim)


def own_rows(running, axes):
    count = lax.axis_size(axes)
    parts = running.astype(jnp.bfloat16).reshape(count, running.shape[0] // count, running.shape[1])
    return jnp.sum(lax.all_to_all(parts, axes, 0, 0, tiled=True).astype(jnp.float32), axis=0)


def pair_mean(table):
    paired = table.reshape(table.shape[0], table.shape[1] // 2, 2, table.shape[2])
    return (paired[:, :, 0] + paired[:, :, 1]) * 0.5


def spread_rows(table):
    doubled = jnp.broadcast_to(
        table[:, :, None], (table.shape[0], table.shape[1], 2, table.shape[2])
    )
    return doubled.reshape(table.shape[0], table.shape[1] * 2, table.shape[2])


def top_bit(d):
    total = jnp.zeros_like(d) - 1
    for k in range(0, 7):
        total = total + (d >= (1 << k)).astype(d.dtype)
    return total


def pooled(table, factor):
    return table.reshape(table.shape[0], table.shape[1] // factor, factor, table.shape[2]).mean(axis=2)


def pad_rows(x, rows):
    return jnp.pad(x, ((0, 0), (0, rows - x.shape[1]), (0, 0)))


def pick_level(level_of, tables, lo):
    out = tables[-1]
    for i in range(len(tables) - 2, -1, -1):
        mask = (level_of == lo + i).reshape((-1,) + (1,) * (tables[i].ndim - 1))
        out = jnp.where(mask, tables[i], out)
    return out


def sibling_rows(recv, start, level, rows):
    count = 1 << level
    part = lax.dynamic_slice_in_dim(recv, start, count, axis=0)[:, :, :rows]
    part = jnp.moveaxis(part, 0, 1)
    return part.reshape(part.shape[0], count * rows, part.shape[3])


def swap_major(block, axis, bit):
    count = lax.axis_size(axis)
    return lax.ppermute(block, axis, [(i, i ^ (1 << bit)) for i in range(count)])


def on_device(queries, keys, values, cotangent, out_weight):
    tokens = queries.shape[0]
    width = queries.shape[1]
    heads = width // HEAD
    coarse = tokens // 2
    scale = 1.0 / math.sqrt(HEAD)
    depth = lax.axis_size(SEQ).bit_length() - 1
    position = lax.axis_index(SEQ)
    major, minor = SEQ
    n_minor = lax.axis_size(minor)
    minor_depth = n_minor.bit_length() - 1
    minor_pos = lax.axis_index(minor)
    major_pos = lax.axis_index(major)
    table = jnp.stack([keys, values]).astype(jnp.float32)
    means = []
    running = table
    for m in range(depth):
        running = pair_mean(running)
        means.append(running.astype(jnp.bfloat16))
    peers = jnp.arange(n_minor, dtype=jnp.int32)
    near_level = top_bit(minor_pos ^ peers)
    near_kv = pick_level(
        near_level,
        [jnp.broadcast_to(pad_rows(means[m], coarse)[None], (n_minor, 2, coarse, width)) for m in range(minor_depth)],
        0,
    )
    upper = jnp.concatenate(means[minor_depth:], axis=1)
    near_send = jnp.concatenate(
        [near_kv, jnp.broadcast_to(upper[None], (n_minor,) + upper.shape)], axis=2
    )
    near_recv = lax.all_to_all(near_send, minor, 0, 0, tiled=True)
    levels_kv = []
    for m in range(minor_depth):
        start = ((minor_pos >> m) ^ 1) << m
        levels_kv.append(sibling_rows(near_recv[:, :, :coarse], start, m, coarse >> m))
    slices = []
    offset = coarse
    for m in range(minor_depth, depth):
        rows = coarse >> m
        part = jnp.moveaxis(near_recv[:, :, offset : offset + rows], 0, 1)
        slices.append(part.reshape(2, n_minor * rows, width))
        offset += rows
    for r in range(depth - minor_depth):
        got = swap_major(jnp.concatenate(slices, axis=1), major, r)
        levels_kv.append(got[:, :coarse])
        lower_half = (major_pos >> r) & 1 == 0
        joined = []
        used = coarse
        for own in slices[1:]:
            far = got[:, used : used + own.shape[1]]
            used += own.shape[1]
            joined.append(
                jnp.where(lower_half, jnp.concatenate([own, far], 1), jnp.concatenate([far, own], 1))
            )
        slices = joined
    key_set = jnp.concatenate([keys] + [lv[0] for lv in levels_kv], axis=0)
    value_set = jnp.concatenate([values] + [lv[1] for lv in levels_kv], axis=0)
    full_cot = gathered_copies(cotangent, "dp", 1)
    full_weight = gathered_copies(out_weight, SEQ, 0)
    grad_attended = jnp.dot(full_cot, full_weight, preferred_element_type=jnp.float32).astype(
        jnp.bfloat16
    )
    attended_parts = []
    grad_query_parts = []
    grad_key_parts = []
    grad_value_parts = []
    for head in range(heads):
        low = head * HEAD
        high = low + HEAD
        query_head = queries[:, low:high]
        key_head = key_set[:, low:high]
        value_head = value_set[:, low:high]
        grad_head = grad_attended[:, low:high]
        scores = (
            jnp.einsum("ta,ka->tk", query_head, key_head, preferred_element_type=jnp.float32)
            * scale
        )
        peak = jnp.max(scores, axis=-1, keepdims=True)
        expo = jnp.exp(scores - peak)
        prob = expo / jnp.sum(expo, axis=-1, keepdims=True)
        weights = prob.astype(jnp.bfloat16)
        attended_parts.append(
            jnp.dot(weights, value_head, preferred_element_type=jnp.float32).astype(jnp.bfloat16)
        )
        grad_weights = jnp.einsum(
            "ta,ka->tk", grad_head, value_head, preferred_element_type=jnp.float32
        )
        delta = jnp.sum(prob * grad_weights, axis=-1, keepdims=True)
        grad_scores = (prob * (grad_weights - delta) * scale).astype(jnp.bfloat16)
        grad_query_parts.append(
            jnp.dot(grad_scores, key_head, preferred_element_type=jnp.float32).astype(jnp.bfloat16)
        )
        grad_key_parts.append(
            jnp.einsum("tk,ta->ka", grad_scores, query_head, preferred_element_type=jnp.float32)
        )
        grad_value_parts.append(
            jnp.einsum("tk,ta->ka", weights, grad_head, preferred_element_type=jnp.float32)
        )
    attended = jnp.concatenate(attended_parts, axis=1)
    grad_queries = jnp.concatenate(grad_query_parts, axis=1)
    grad_sets = jnp.stack(
        [jnp.concatenate(grad_key_parts, axis=1), jnp.concatenate(grad_value_parts, axis=1)]
    )
    carried = jnp.zeros((2, coarse, width), jnp.float32)
    for layer_bit in reversed(range(depth)):
        first = tokens + layer_bit * coarse
        outgoing = grad_sets[:, first : first + coarse]
        kept = jnp.zeros((2, coarse, width), jnp.float32)
        if layer_bit + 1 < depth:
            lower_half = position >> layer_bit & 1 == 0
            spread = spread_rows(carried * 0.5)
            low_part = spread[:, :coarse]
            high_part = spread[:, coarse:]
            kept = jnp.where(lower_half, low_part, high_part)
            outgoing = outgoing + jnp.where(lower_half, high_part, low_part)
        incoming = from_partner(outgoing.astype(jnp.bfloat16), SEQ, layer_bit).astype(
            outgoing.dtype
        )
        carried = kept + incoming
    own_grads = grad_sets[:, :tokens] + spread_rows(carried * 0.5)
    grad_keys = own_grads[0].astype(jnp.bfloat16)
    grad_values = own_grads[1].astype(jnp.bfloat16)
    grad_out_weight = own_rows(
        lax.dot_general(
            full_cot, attended, (((0,), (0,)), ((), ())), preferred_element_type=jnp.float32
        ),
        SEQ,
    )
    return (attended, grad_queries, grad_keys, grad_values, grad_out_weight)


def solution(mesh):
    torus = Mesh(mesh.devices.reshape(8, 8, mesh.shape["dp"]), ("seq_0", "seq_1", "dp"))
    placed = (P(SEQ, "dp"), P(SEQ, "dp"), P(SEQ, "dp"), P(SEQ, "dp"), P(SEQ, "dp"))
    return jax.shard_map(
        on_device,
        mesh=torus,
        in_specs=placed,
        out_specs=(P(SEQ, "dp"), P(SEQ, "dp"), P(SEQ, "dp"), P(SEQ, "dp"), P(SEQ, "dp")),
        check_vma=False,
    )
```

```python
import math

import jax
import jax.numpy as jnp
from jax import lax
from jax.sharding import Mesh
from jax.sharding import PartitionSpec as P

HEAD = 128
SEQ = ("seq_0", "seq_1")


def from_partner(block, axis, apart):
    count = lax.axis_size(axis)
    route = []
    for low in range(count):
        high = low | 1 << apart
        if high != low and high < count:
            route += [(low, high), (high, low)]
    return lax.ppermute(block, axis, route)


def joined_along(blocks, dim):
    blocks = jnp.moveaxis(blocks, 0, dim)
    dims = blocks.shape
    return blocks.reshape(*dims[:dim], dims[dim] * dims[dim + 1], *dims[dim + 2 :])


def from_everyone(x, axis):
    copies = jnp.broadcast_to(x, (lax.axis_size(axis), *x.shape))
    return lax.all_to_all(copies, axis, split_axis=0, concat_axis=0, tiled=True)


def gathered_copies(x, axis, dim):
    return joined_along(from_everyone(x, axis), dim)


def own_rows(running, axes):
    count = lax.axis_size(axes)
    parts = running.astype(jnp.bfloat16).reshape(count, running.shape[0] // count, running.shape[1])
    return jnp.sum(lax.all_to_all(parts, axes, 0, 0, tiled=True).astype(jnp.float32), axis=0)


def pair_mean(table):
    paired = table.reshape(table.shape[0], table.shape[1] // 2, 2, table.shape[2])
    return (paired[:, :, 0] + paired[:, :, 1]) * 0.5


def spread_rows(table):
    doubled = jnp.broadcast_to(
        table[:, :, None], (table.shape[0], table.shape[1], 2, table.shape[2])
    )
    return doubled.reshape(table.shape[0], table.shape[1] * 2, table.shape[2])


def top_bit(d):
    total = jnp.zeros_like(d) - 1
    for k in range(0, 7):
        total = total + (d >= (1 << k)).astype(d.dtype)
    return total


def pad_rows(x, rows):
    return jnp.pad(x, ((0, 0), (0, rows - x.shape[1]), (0, 0)))


def pick_level(level_of, tables, lo):
    out = tables[-1]
    for i in range(len(tables) - 2, -1, -1):
        mask = (level_of == lo + i).reshape((-1,) + (1,) * (tables[i].ndim - 1))
        out = jnp.where(mask, tables[i], out)
    return out


def on_device(queries, keys, values, cotangent, out_weight):
    tokens = queries.shape[0]
    width = queries.shape[1]
    heads = width // HEAD
    coarse = tokens // 2
    scale = 1.0 / math.sqrt(HEAD)
    depth = lax.axis_size(SEQ).bit_length() - 1
    position = lax.axis_index(SEQ)
    own_table = pair_mean(jnp.stack([keys, values]).astype(jnp.float32))
    far_keys = []
    far_values = []
    for layer_bit in range(depth):
        far_table = from_partner(own_table, SEQ, layer_bit)
        far_keys.append(far_table[0].astype(jnp.bfloat16))
        far_values.append(far_table[1].astype(jnp.bfloat16))
        if layer_bit + 1 < depth:
            lower_half = position >> layer_bit & 1 == 0
            joined = jnp.concatenate(
                [
                    jnp.where(lower_half, own_table, far_table),
                    jnp.where(lower_half, far_table, own_table),
                ],
                axis=1,
            )
            own_table = pair_mean(joined)
    key_set = jnp.concatenate([keys] + far_keys, axis=0)
    value_set = jnp.concatenate([values] + far_values, axis=0)
    full_cot = gathered_copies(cotangent, "dp", 1)
    full_weight = gathered_copies(out_weight, SEQ, 0)
    grad_attended = jnp.dot(full_cot, full_weight, preferred_element_type=jnp.float32).astype(
        jnp.bfloat16
    )
    attended_parts = []
    grad_query_parts = []
    grad_key_parts = []
    grad_value_parts = []
    for head in range(heads):
        low = head * HEAD
        high = low + HEAD
        query_head = queries[:, low:high]
        key_head = key_set[:, low:high]
        value_head = value_set[:, low:high]
        grad_head = grad_attended[:, low:high]
        scores = (
            jnp.einsum("ta,ka->tk", query_head, key_head, preferred_element_type=jnp.float32)
            * scale
        )
        peak = jnp.max(scores, axis=-1, keepdims=True)
        expo = jnp.exp(scores - peak)
        prob = expo / jnp.sum(expo, axis=-1, keepdims=True)
        weights = prob.astype(jnp.bfloat16)
        attended_parts.append(
            jnp.dot(weights, value_head, preferred_element_type=jnp.float32).astype(jnp.bfloat16)
        )
        grad_weights = jnp.einsum(
            "ta,ka->tk", grad_head, value_head, preferred_element_type=jnp.float32
        )
        delta = jnp.sum(prob * grad_weights, axis=-1, keepdims=True)
        grad_scores = (prob * (grad_weights - delta) * scale).astype(jnp.bfloat16)
        grad_query_parts.append(
            jnp.dot(grad_scores, key_head, preferred_element_type=jnp.float32).astype(jnp.bfloat16)
        )
        grad_key_parts.append(
            jnp.einsum("tk,ta->ka", grad_scores, query_head, preferred_element_type=jnp.float32)
        )
        grad_value_parts.append(
            jnp.einsum("tk,ta->ka", weights, grad_head, preferred_element_type=jnp.float32)
        )
    attended = jnp.concatenate(attended_parts, axis=1)
    grad_queries = jnp.concatenate(grad_query_parts, axis=1)
    grad_sets = jnp.stack(
        [jnp.concatenate(grad_key_parts, axis=1), jnp.concatenate(grad_value_parts, axis=1)]
    )
    major, minor = SEQ
    n_minor = lax.axis_size(minor)
    n_seq = lax.axis_size(SEQ)
    minor_depth = n_minor.bit_length() - 1
    far_rows = coarse >> minor_depth
    near_level = top_bit(lax.axis_index(minor) ^ jnp.arange(n_minor, dtype=jnp.int32))
    far_level = top_bit(position ^ jnp.arange(n_seq, dtype=jnp.int32))
    level_grads = []
    for m in range(depth):
        first = tokens + m * coarse
        part = grad_sets[:, first : first + coarse].astype(jnp.bfloat16)
        level_grads.append(part.reshape(2, 1 << m, coarse >> m, width))
    near_back = pick_level(
        near_level,
        [
            jnp.stack([pad_rows(level_grads[m][:, k & ((1 << m) - 1)], coarse) for k in range(n_minor)])
            for m in range(minor_depth)
        ],
        0,
    )
    near_got = lax.all_to_all(near_back, minor, 0, 0, tiled=True).astype(jnp.float32)
    far_back = pick_level(
        far_level,
        [
            jnp.stack([pad_rows(level_grads[m][:, c & ((1 << m) - 1)], far_rows) for c in range(n_seq)])
            for m in range(minor_depth, depth)
        ],
        minor_depth,
    )
    weight_grad = lax.dot_general(
        full_cot, attended, (((0,), (0,)), ((), ())), preferred_element_type=jnp.float32
    )
    w_rows = weight_grad.shape[0] // n_seq
    far_send = jnp.concatenate(
        [
            far_back.reshape(n_seq, 2 * far_rows, width),
            weight_grad.astype(jnp.bfloat16).reshape(n_seq, w_rows, width),
        ],
        axis=1,
    )
    far_all = lax.all_to_all(far_send, SEQ, 0, 0, tiled=True).astype(jnp.float32)
    far_got = far_all[:, : 2 * far_rows].reshape(n_seq, 2, far_rows, width)
    grad_out_weight = jnp.sum(far_all[:, 2 * far_rows :], axis=0)

    own_grads = grad_sets[:, :tokens]
    for m in range(depth):
        rows = coarse >> m
        if m < minor_depth:
            got, level_of = near_got, near_level
        else:
            got, level_of = far_got, far_level
        mask = (level_of == m).reshape(-1, 1, 1, 1)
        summed = jnp.sum(jnp.where(mask, got[:, :, :rows], 0.0), axis=0)
        factor = 2 << m
        spread = jnp.broadcast_to((summed / factor)[:, :, None], (2, rows, factor, width))
        own_grads = own_grads + spread.reshape(2, tokens, width)
    grad_keys = own_grads[0].astype(jnp.bfloat16)
    grad_values = own_grads[1].astype(jnp.bfloat16)
    return (attended, grad_queries, grad_keys, grad_values, grad_out_weight)


def solution(mesh):
    torus = Mesh(mesh.devices.reshape(8, 8, mesh.shape["dp"]), ("seq_0", "seq_1", "dp"))
    placed = (P(SEQ, "dp"), P(SEQ, "dp"), P(SEQ, "dp"), P(SEQ, "dp"), P(SEQ, "dp"))
    return jax.shard_map(
        on_device,
        mesh=torus,
        in_specs=placed,
        out_specs=(P(SEQ, "dp"), P(SEQ, "dp"), P(SEQ, "dp"), P(SEQ, "dp"), P(SEQ, "dp")),
        check_vma=False,
    )
```

```python
import math

import jax
import jax.numpy as jnp
from jax import lax
from jax.sharding import Mesh
from jax.sharding import PartitionSpec as P

HEAD = 128
SEQ = ("seq_0", "seq_1")


def from_partner(block, axis, apart):
    count = lax.axis_size(axis)
    route = []
    for low in range(count):
        high = low | 1 << apart
        if high != low and high < count:
            route += [(low, high), (high, low)]
    return lax.ppermute(block, axis, route)


def joined_along(blocks, dim):
    blocks = jnp.moveaxis(blocks, 0, dim)
    dims = blocks.shape
    return blocks.reshape(*dims[:dim], dims[dim] * dims[dim + 1], *dims[dim + 2 :])


def from_everyone(x, axis):
    copies = jnp.broadcast_to(x, (lax.axis_size(axis), *x.shape))
    return lax.all_to_all(copies, axis, split_axis=0, concat_axis=0, tiled=True)


def gathered_copies(x, axis, dim):
    return joined_along(from_everyone(x, axis), dim)


def own_rows(running, axes):
    count = lax.axis_size(axes)
    parts = running.astype(jnp.bfloat16).reshape(count, running.shape[0] // count, running.shape[1])
    return jnp.sum(lax.all_to_all(parts, axes, 0, 0, tiled=True).astype(jnp.float32), axis=0)


def pair_mean(table):
    paired = table.reshape(table.shape[0], table.shape[1] // 2, 2, table.shape[2])
    return (paired[:, :, 0] + paired[:, :, 1]) * 0.5


def pair_mean_rows(table, factor):
    return table.reshape(table.shape[0], table.shape[1] // factor, factor, table.shape[2]).mean(axis=2)


def spread_rows(table):
    doubled = jnp.broadcast_to(
        table[:, :, None], (table.shape[0], table.shape[1], 2, table.shape[2])
    )
    return doubled.reshape(table.shape[0], table.shape[1] * 2, table.shape[2])


def on_device(queries, keys, values, cotangent, out_weight):
    tokens = queries.shape[0]
    width = queries.shape[1]
    heads = width // HEAD
    coarse = tokens // 2
    scale = 1.0 / math.sqrt(HEAD)
    depth = lax.axis_size(SEQ).bit_length() - 1
    position = lax.axis_index(SEQ)
    own_table = pair_mean(jnp.stack([keys, values]).astype(jnp.float32))
    far_keys = []
    far_values = []
    top = depth - 1
    top_rows = pair_mean_rows(jnp.stack([keys, values]).astype(jnp.float32), 2 << top).astype(jnp.bfloat16)
    n_seq = lax.axis_size(SEQ)
    w_rows = out_weight.shape[0]
    top_count = top_rows.shape[1]
    send = jnp.concatenate(
        [
            jnp.broadcast_to(out_weight[None], (n_seq, w_rows, width)),
            jnp.broadcast_to(top_rows.reshape(1, 2 * top_count, width), (n_seq, 2 * top_count, width)),
        ],
        axis=1,
    )
    arrived = lax.all_to_all(send, SEQ, 0, 0, tiled=True)
    full_weight = arrived[:, :w_rows].reshape(n_seq * w_rows, width)
    first = ((position >> top) ^ 1) << top
    top_far = lax.dynamic_slice_in_dim(arrived[:, w_rows:], first, 1 << top, axis=0)
    top_far = top_far.reshape(1 << top, 2, top_count, width)
    for layer_bit in range(depth):
        if layer_bit == top:
            far_keys.append(top_far[:, 0].reshape(-1, width))
            far_values.append(top_far[:, 1].reshape(-1, width))
            continue
        far_table = from_partner(own_table, SEQ, layer_bit)
        far_keys.append(far_table[0].astype(jnp.bfloat16))
        far_values.append(far_table[1].astype(jnp.bfloat16))
        if layer_bit + 1 < depth:
            lower_half = position >> layer_bit & 1 == 0
            joined = jnp.concatenate(
                [
                    jnp.where(lower_half, own_table, far_table),
                    jnp.where(lower_half, far_table, own_table),
                ],
                axis=1,
            )
            own_table = pair_mean(joined)
    key_set = jnp.concatenate([keys] + far_keys, axis=0)
    value_set = jnp.concatenate([values] + far_values, axis=0)
    full_cot = gathered_copies(cotangent, "dp", 1)
    grad_attended = jnp.dot(full_cot, full_weight, preferred_element_type=jnp.float32).astype(
        jnp.bfloat16
    )
    attended_parts = []
    grad_query_parts = []
    grad_key_parts = []
    grad_value_parts = []
    for head in range(heads):
        low = head * HEAD
        high = low + HEAD
        query_head = queries[:, low:high]
        key_head = key_set[:, low:high]
        value_head = value_set[:, low:high]
        grad_head = grad_attended[:, low:high]
        scores = (
            jnp.einsum("ta,ka->tk", query_head, key_head, preferred_element_type=jnp.float32)
            * scale
        )
        peak = jnp.max(scores, axis=-1, keepdims=True)
        expo = jnp.exp(scores - peak)
        prob = expo / jnp.sum(expo, axis=-1, keepdims=True)
        weights = prob.astype(jnp.bfloat16)
        attended_parts.append(
            jnp.dot(weights, value_head, preferred_element_type=jnp.float32).astype(jnp.bfloat16)
        )
        grad_weights = jnp.einsum(
            "ta,ka->tk", grad_head, value_head, preferred_element_type=jnp.float32
        )
        delta = jnp.sum(prob * grad_weights, axis=-1, keepdims=True)
        grad_scores = (prob * (grad_weights - delta) * scale).astype(jnp.bfloat16)
        grad_query_parts.append(
            jnp.dot(grad_scores, key_head, preferred_element_type=jnp.float32).astype(jnp.bfloat16)
        )
        grad_key_parts.append(
            jnp.einsum("tk,ta->ka", grad_scores, query_head, preferred_element_type=jnp.float32)
        )
        grad_value_parts.append(
            jnp.einsum("tk,ta->ka", weights, grad_head, preferred_element_type=jnp.float32)
        )
    attended = jnp.concatenate(attended_parts, axis=1)
    grad_queries = jnp.concatenate(grad_query_parts, axis=1)
    grad_sets = jnp.stack(
        [jnp.concatenate(grad_key_parts, axis=1), jnp.concatenate(grad_value_parts, axis=1)]
    )
    carried = jnp.zeros((2, coarse, width), jnp.float32)
    for layer_bit in reversed(range(depth)):
        first = tokens + layer_bit * coarse
        outgoing = grad_sets[:, first : first + coarse]
        kept = jnp.zeros((2, coarse, width), jnp.float32)
        if layer_bit + 1 < depth:
            lower_half = position >> layer_bit & 1 == 0
            spread = spread_rows(carried * 0.5)
            low_part = spread[:, :coarse]
            high_part = spread[:, coarse:]
            kept = jnp.where(lower_half, low_part, high_part)
            outgoing = outgoing + jnp.where(lower_half, high_part, low_part)
        incoming = from_partner(outgoing.astype(jnp.bfloat16), SEQ, layer_bit).astype(
            outgoing.dtype
        )
        carried = kept + incoming
    own_grads = grad_sets[:, :tokens] + spread_rows(carried * 0.5)
    grad_keys = own_grads[0].astype(jnp.bfloat16)
    grad_values = own_grads[1].astype(jnp.bfloat16)
    grad_out_weight = own_rows(
        lax.dot_general(
            full_cot, attended, (((0,), (0,)), ((), ())), preferred_element_type=jnp.float32
        ),
        SEQ,
    )
    return (attended, grad_queries, grad_keys, grad_values, grad_out_weight)


def solution(mesh):
    torus = Mesh(mesh.devices.reshape(8, 8, mesh.shape["dp"]), ("seq_0", "seq_1", "dp"))
    placed = (P(SEQ, "dp"), P(SEQ, "dp"), P(SEQ, "dp"), P(SEQ, "dp"), P(SEQ, "dp"))
    return jax.shard_map(
        on_device,
        mesh=torus,
        in_specs=placed,
        out_specs=(P(SEQ, "dp"), P(SEQ, "dp"), P(SEQ, "dp"), P(SEQ, "dp"), P(SEQ, "dp")),
        check_vma=False,
    )
```

```python
import math

import jax
import jax.numpy as jnp
from jax import lax
from jax.sharding import Mesh
from jax.sharding import PartitionSpec as P

HEAD = 128
SEQ = ("seq_0", "seq_1")


def from_partner(block, axis, apart):
    count = lax.axis_size(axis)
    route = []
    for low in range(count):
        high = low | 1 << apart
        if high != low and high < count:
            route += [(low, high), (high, low)]
    return lax.ppermute(block, axis, route)


def joined_along(blocks, dim):
    blocks = jnp.moveaxis(blocks, 0, dim)
    dims = blocks.shape
    return blocks.reshape(*dims[:dim], dims[dim] * dims[dim + 1], *dims[dim + 2 :])


def from_everyone(x, axis):
    copies = jnp.broadcast_to(x, (lax.axis_size(axis), *x.shape))
    return lax.all_to_all(copies, axis, split_axis=0, concat_axis=0, tiled=True)


def gathered_copies(x, axis, dim):
    return joined_along(from_everyone(x, axis), dim)


def own_rows(running, axes):
    count = lax.axis_size(axes)
    parts = running.astype(jnp.bfloat16).reshape(count, running.shape[0] // count, running.shape[1])
    return jnp.sum(lax.all_to_all(parts, axes, 0, 0, tiled=True).astype(jnp.float32), axis=0)


def pair_mean(table):
    paired = table.reshape(table.shape[0], table.shape[1] // 2, 2, table.shape[2])
    return (paired[:, :, 0] + paired[:, :, 1]) * 0.5


def spread_rows(table):
    doubled = jnp.broadcast_to(
        table[:, :, None], (table.shape[0], table.shape[1], 2, table.shape[2])
    )
    return doubled.reshape(table.shape[0], table.shape[1] * 2, table.shape[2])


def on_device(queries, keys, values, cotangent, out_weight):
    tokens = queries.shape[0]
    width = queries.shape[1]
    heads = width // HEAD
    coarse = tokens // 2
    scale = 1.0 / math.sqrt(HEAD)
    depth = lax.axis_size(SEQ).bit_length() - 1
    position = lax.axis_index(SEQ)
    own_table = jnp.stack(
        [pair_mean(keys[None].astype(jnp.float32))[0], pair_mean(values[None].astype(jnp.float32))[0]]
    )
    far_keys = []
    far_values = []
    for layer_bit in range(depth):
        far_table = from_partner(own_table, SEQ, layer_bit)
        far_keys.append(far_table[0].astype(jnp.bfloat16))
        far_values.append(far_table[1].astype(jnp.bfloat16))
        if layer_bit + 1 < depth:
            lower_half = position >> layer_bit & 1 == 0
            joined = jnp.concatenate(
                [
                    jnp.where(lower_half, own_table, far_table),
                    jnp.where(lower_half, far_table, own_table),
                ],
                axis=1,
            )
            own_table = pair_mean(joined)
    key_set = jnp.concatenate([keys] + far_keys, axis=0)
    value_set = jnp.concatenate([values] + far_values, axis=0)
    full_cot = gathered_copies(cotangent, "dp", 1)
    full_weight = gathered_copies(out_weight, SEQ, 0)
    grad_attended = jnp.dot(full_cot, full_weight, preferred_element_type=jnp.float32).astype(
        jnp.bfloat16
    )
    attended_parts = []
    grad_query_parts = []
    grad_key_parts = []
    grad_value_parts = []
    for head in range(heads):
        low = head * HEAD
        high = low + HEAD
        query_head = queries[:, low:high]
        key_head = key_set[:, low:high]
        value_head = value_set[:, low:high]
        grad_head = grad_attended[:, low:high]
        scores = (
            jnp.einsum("ta,ka->tk", query_head, key_head, preferred_element_type=jnp.float32)
            * scale
        )
        peak = jnp.max(scores, axis=-1, keepdims=True)
        expo = jnp.exp(scores - peak)
        prob = expo / jnp.sum(expo, axis=-1, keepdims=True)
        weights = prob.astype(jnp.bfloat16)
        attended_parts.append(
            jnp.dot(weights, value_head, preferred_element_type=jnp.float32).astype(jnp.bfloat16)
        )
        grad_weights = jnp.einsum(
            "ta,ka->tk", grad_head, value_head, preferred_element_type=jnp.float32
        )
        delta = jnp.sum(prob * grad_weights, axis=-1, keepdims=True)
        grad_scores = (prob * (grad_weights - delta) * scale).astype(jnp.bfloat16)
        grad_query_parts.append(
            jnp.dot(grad_scores, key_head, preferred_element_type=jnp.float32).astype(jnp.bfloat16)
        )
        grad_key_parts.append(
            jnp.einsum("tk,ta->ka", grad_scores, query_head, preferred_element_type=jnp.float32)
        )
        grad_value_parts.append(
            jnp.einsum("tk,ta->ka", weights, grad_head, preferred_element_type=jnp.float32)
        )
    attended = jnp.concatenate(attended_parts, axis=1)
    grad_queries = jnp.concatenate(grad_query_parts, axis=1)
    grad_sets = jnp.stack(
        [jnp.concatenate(grad_key_parts, axis=1), jnp.concatenate(grad_value_parts, axis=1)]
    )
    carried = jnp.zeros((2, coarse, width), jnp.float32)
    for layer_bit in reversed(range(depth)):
        first = tokens + layer_bit * coarse
        outgoing = grad_sets[:, first : first + coarse]
        kept = jnp.zeros((2, coarse, width), jnp.float32)
        if layer_bit + 1 < depth:
            lower_half = position >> layer_bit & 1 == 0
            spread = spread_rows(carried * 0.5)
            low_part = spread[:, :coarse]
            high_part = spread[:, coarse:]
            kept = jnp.where(lower_half, low_part, high_part)
            outgoing = outgoing + jnp.where(lower_half, high_part, low_part)
        incoming = from_partner(outgoing.astype(jnp.bfloat16), SEQ, layer_bit).astype(
            outgoing.dtype
        )
        carried = kept + incoming
    own_grads = grad_sets[:, :tokens] + spread_rows(carried * 0.5)
    grad_keys = own_grads[0].astype(jnp.bfloat16)
    grad_values = own_grads[1].astype(jnp.bfloat16)
    grad_out_weight = own_rows(
        lax.dot_general(
            full_cot, attended, (((0,), (0,)), ((), ())), preferred_element_type=jnp.bfloat16
        ),
        SEQ,
    )
    return (attended, grad_queries, grad_keys, grad_values, grad_out_weight)


def solution(mesh):
    torus = Mesh(mesh.devices.reshape(8, 8, mesh.shape["dp"]), ("seq_0", "seq_1", "dp"))
    placed = (P(SEQ, "dp"), P(SEQ, "dp"), P(SEQ, "dp"), P(SEQ, "dp"), P(SEQ, "dp"))
    return jax.shard_map(
        on_device,
        mesh=torus,
        in_specs=placed,
        out_specs=(P(SEQ, "dp"), P(SEQ, "dp"), P(SEQ, "dp"), P(SEQ, "dp"), P(SEQ, "dp")),
        check_vma=False,
    )
```

```python
import math

import jax
import jax.numpy as jnp
from jax import lax
from jax.sharding import Mesh
from jax.sharding import PartitionSpec as P

HEAD = 128
SEQ = ("seq_0", "seq_1")


def from_partner(block, axis, apart):
    count = lax.axis_size(axis)
    route = []
    for low in range(count):
        high = low | 1 << apart
        if high != low and high < count:
            route += [(low, high), (high, low)]
    return lax.ppermute(block, axis, route)


def joined_along(blocks, dim):
    blocks = jnp.moveaxis(blocks, 0, dim)
    dims = blocks.shape
    return blocks.reshape(*dims[:dim], dims[dim] * dims[dim + 1], *dims[dim + 2 :])


def from_everyone(x, axis):
    copies = jnp.broadcast_to(x, (lax.axis_size(axis), *x.shape))
    return lax.all_to_all(copies, axis, split_axis=0, concat_axis=0, tiled=True)


def gathered_copies(x, axis, dim):
    return joined_along(from_everyone(x, axis), dim)


def own_rows(running, axes):
    count = lax.axis_size(axes)
    parts = running.astype(jnp.bfloat16).reshape(count, running.shape[0] // count, running.shape[1])
    return jnp.sum(lax.all_to_all(parts, axes, 0, 0, tiled=True).astype(jnp.float32), axis=0)


def pair_mean(table):
    paired = table.reshape(table.shape[0], table.shape[1] // 2, 2, table.shape[2])
    return (paired[:, :, 0] + paired[:, :, 1]) * 0.5


def pair_mean_rows(table, factor):
    return table.reshape(table.shape[0], table.shape[1] // factor, factor, table.shape[2]).mean(axis=2)


def spread_rows(table):
    doubled = jnp.broadcast_to(
        table[:, :, None], (table.shape[0], table.shape[1], 2, table.shape[2])
    )
    return doubled.reshape(table.shape[0], table.shape[1] * 2, table.shape[2])


def on_device(queries, keys, values, cotangent, out_weight):
    tokens = queries.shape[0]
    width = queries.shape[1]
    heads = width // HEAD
    coarse = tokens // 2
    scale = 1.0 / math.sqrt(HEAD)
    depth = lax.axis_size(SEQ).bit_length() - 1
    position = lax.axis_index(SEQ)
    own_table = pair_mean(jnp.stack([keys, values]).astype(jnp.float32))
    far_keys = []
    far_values = []
    top = depth - 1
    top_rows = pair_mean_rows(jnp.stack([keys, values]).astype(jnp.float32), 2 << top).astype(jnp.bfloat16)
    n_seq = lax.axis_size(SEQ)
    w_rows = out_weight.shape[0]
    top_count = top_rows.shape[1]
    send = jnp.concatenate(
        [
            jnp.broadcast_to(out_weight[None], (n_seq, w_rows, width)),
            jnp.broadcast_to(top_rows.reshape(1, 2 * top_count, width), (n_seq, 2 * top_count, width)),
        ],
        axis=1,
    )
    first = ((position >> top) ^ 1) << top
    tie = max(top - 2, 0)
    for layer_bit in range(depth):
        if layer_bit == top:
            far_keys.append(top_far[:, 0].reshape(-1, width))
            far_values.append(top_far[:, 1].reshape(-1, width))
            continue
        far_table = from_partner(own_table, SEQ, layer_bit)
        if layer_bit == tie:
            send, far_table = lax.optimization_barrier((send, far_table))
            arrived = lax.all_to_all(send, SEQ, 0, 0, tiled=True)
            full_weight = arrived[:, :w_rows].reshape(n_seq * w_rows, width)
            top_far = lax.dynamic_slice_in_dim(arrived[:, w_rows:], first, 1 << top, axis=0)
            top_far = top_far.reshape(1 << top, 2, top_count, width)
        far_keys.append(far_table[0].astype(jnp.bfloat16))
        far_values.append(far_table[1].astype(jnp.bfloat16))
        if layer_bit + 1 < depth:
            lower_half = position >> layer_bit & 1 == 0
            joined = jnp.concatenate(
                [
                    jnp.where(lower_half, own_table, far_table),
                    jnp.where(lower_half, far_table, own_table),
                ],
                axis=1,
            )
            own_table = pair_mean(joined)
    key_set = jnp.concatenate([keys] + far_keys, axis=0)
    value_set = jnp.concatenate([values] + far_values, axis=0)
    full_cot = gathered_copies(cotangent, "dp", 1)
    grad_attended = jnp.dot(full_cot, full_weight, preferred_element_type=jnp.float32).astype(
        jnp.bfloat16
    )
    attended_parts = []
    grad_query_parts = []
    grad_key_parts = []
    grad_value_parts = []
    for head in range(heads):
        low = head * HEAD
        high = low + HEAD
        query_head = queries[:, low:high]
        key_head = key_set[:, low:high]
        value_head = value_set[:, low:high]
        grad_head = grad_attended[:, low:high]
        scores = (
            jnp.einsum("ta,ka->tk", query_head, key_head, preferred_element_type=jnp.float32)
            * scale
        )
        peak = jnp.max(scores, axis=-1, keepdims=True)
        expo = jnp.exp(scores - peak)
        prob = expo / jnp.sum(expo, axis=-1, keepdims=True)
        weights = prob.astype(jnp.bfloat16)
        attended_parts.append(
            jnp.dot(weights, value_head, preferred_element_type=jnp.float32).astype(jnp.bfloat16)
        )
        grad_weights = jnp.einsum(
            "ta,ka->tk", grad_head, value_head, preferred_element_type=jnp.float32
        )
        delta = jnp.sum(prob * grad_weights, axis=-1, keepdims=True)
        grad_scores = (prob * (grad_weights - delta) * scale).astype(jnp.bfloat16)
        grad_query_parts.append(
            jnp.dot(grad_scores, key_head, preferred_element_type=jnp.float32).astype(jnp.bfloat16)
        )
        grad_key_parts.append(
            jnp.einsum("tk,ta->ka", grad_scores, query_head, preferred_element_type=jnp.float32)
        )
        grad_value_parts.append(
            jnp.einsum("tk,ta->ka", weights, grad_head, preferred_element_type=jnp.float32)
        )
    attended = jnp.concatenate(attended_parts, axis=1)
    grad_queries = jnp.concatenate(grad_query_parts, axis=1)
    grad_sets = jnp.stack(
        [jnp.concatenate(grad_key_parts, axis=1), jnp.concatenate(grad_value_parts, axis=1)]
    )
    carried = jnp.zeros((2, coarse, width), jnp.float32)
    for layer_bit in reversed(range(depth)):
        first = tokens + layer_bit * coarse
        outgoing = grad_sets[:, first : first + coarse]
        kept = jnp.zeros((2, coarse, width), jnp.float32)
        if layer_bit + 1 < depth:
            lower_half = position >> layer_bit & 1 == 0
            spread = spread_rows(carried * 0.5)
            low_part = spread[:, :coarse]
            high_part = spread[:, coarse:]
            kept = jnp.where(lower_half, low_part, high_part)
            outgoing = outgoing + jnp.where(lower_half, high_part, low_part)
        incoming = from_partner(outgoing.astype(jnp.bfloat16), SEQ, layer_bit).astype(
            outgoing.dtype
        )
        carried = kept + incoming
    own_grads = grad_sets[:, :tokens] + spread_rows(carried * 0.5)
    grad_keys = own_grads[0].astype(jnp.bfloat16)
    grad_values = own_grads[1].astype(jnp.bfloat16)
    grad_out_weight = own_rows(
        lax.dot_general(
            full_cot, attended, (((0,), (0,)), ((), ())), preferred_element_type=jnp.float32
        ),
        SEQ,
    )
    return (attended, grad_queries, grad_keys, grad_values, grad_out_weight)


def solution(mesh):
    torus = Mesh(mesh.devices.reshape(8, 8, mesh.shape["dp"]), ("seq_0", "seq_1", "dp"))
    placed = (P(SEQ, "dp"), P(SEQ, "dp"), P(SEQ, "dp"), P(SEQ, "dp"), P(SEQ, "dp"))
    return jax.shard_map(
        on_device,
        mesh=torus,
        in_specs=placed,
        out_specs=(P(SEQ, "dp"), P(SEQ, "dp"), P(SEQ, "dp"), P(SEQ, "dp"), P(SEQ, "dp")),
        check_vma=False,
    )
```

```python
import math

import jax
import jax.numpy as jnp
from jax import lax
from jax.sharding import Mesh
from jax.sharding import PartitionSpec as P

HEAD = 128
SEQ = ("seq_0", "seq_1")


def from_partner(block, axis, apart):
    count = lax.axis_size(axis)
    route = []
    for low in range(count):
        high = low | 1 << apart
        if high != low and high < count:
            route += [(low, high), (high, low)]
    return lax.ppermute(block, axis, route)


def joined_along(blocks, dim):
    blocks = jnp.moveaxis(blocks, 0, dim)
    dims = blocks.shape
    return blocks.reshape(*dims[:dim], dims[dim] * dims[dim + 1], *dims[dim + 2 :])


def from_everyone(x, axis):
    copies = jnp.broadcast_to(x, (lax.axis_size(axis), *x.shape))
    return lax.all_to_all(copies, axis, split_axis=0, concat_axis=0, tiled=True)


def gathered_copies(x, axis, dim):
    return joined_along(from_everyone(x, axis), dim)


def own_rows(running, axes):
    count = lax.axis_size(axes)
    parts = running.astype(jnp.bfloat16).reshape(count, running.shape[0] // count, running.shape[1])
    return jnp.sum(lax.all_to_all(parts, axes, 0, 0, tiled=True).astype(jnp.float32), axis=0)


def pair_mean(table):
    paired = table.reshape(table.shape[0], table.shape[1] // 2, 2, table.shape[2])
    return (paired[:, :, 0] + paired[:, :, 1]) * 0.5


def spread_rows(table):
    doubled = jnp.broadcast_to(
        table[:, :, None], (table.shape[0], table.shape[1], 2, table.shape[2])
    )
    return doubled.reshape(table.shape[0], table.shape[1] * 2, table.shape[2])


def on_device(queries, keys, values, cotangent, out_weight):
    tokens = queries.shape[0]
    width = queries.shape[1]
    heads = width // HEAD
    coarse = tokens // 2
    scale = 1.0 / math.sqrt(HEAD)
    depth = lax.axis_size(SEQ).bit_length() - 1
    position = lax.axis_index(SEQ)
    own_table = jnp.stack(
        [pair_mean(keys[None].astype(jnp.float32))[0], pair_mean(values[None].astype(jnp.float32))[0]]
    )
    far_keys = []
    far_values = []
    for layer_bit in range(depth):
        far_table = from_partner(own_table.astype(jnp.bfloat16), SEQ, layer_bit).astype(jnp.float32)
        far_keys.append(far_table[0].astype(jnp.bfloat16))
        far_values.append(far_table[1].astype(jnp.bfloat16))
        if layer_bit + 1 < depth:
            lower_half = position >> layer_bit & 1 == 0
            joined = jnp.concatenate(
                [
                    jnp.where(lower_half, own_table, far_table),
                    jnp.where(lower_half, far_table, own_table),
                ],
                axis=1,
            )
            own_table = pair_mean(joined)
    key_set = jnp.concatenate([keys] + far_keys, axis=0)
    value_set = jnp.concatenate([values] + far_values, axis=0)
    full_cot = gathered_copies(cotangent, "dp", 1)
    full_weight = gathered_copies(out_weight, SEQ, 0)
    grad_attended = jnp.dot(full_cot, full_weight, preferred_element_type=jnp.float32).astype(
        jnp.bfloat16
    )
    attended_parts = []
    grad_query_parts = []
    grad_key_parts = []
    grad_value_parts = []
    for head in range(heads):
        low = head * HEAD
        high = low + HEAD
        query_head = queries[:, low:high]
        key_head = key_set[:, low:high]
        value_head = value_set[:, low:high]
        grad_head = grad_attended[:, low:high]
        scores = (
            jnp.einsum("ta,ka->tk", query_head, key_head, preferred_element_type=jnp.float32)
            * scale
        )
        peak = jnp.max(scores, axis=-1, keepdims=True)
        expo = jnp.exp(scores - peak)
        prob = expo / jnp.sum(expo, axis=-1, keepdims=True)
        weights = prob.astype(jnp.bfloat16)
        attended_parts.append(
            jnp.dot(weights, value_head, preferred_element_type=jnp.float32).astype(jnp.bfloat16)
        )
        grad_weights = jnp.einsum(
            "ta,ka->tk", grad_head, value_head, preferred_element_type=jnp.float32
        )
        delta = jnp.sum(prob * grad_weights, axis=-1, keepdims=True)
        grad_scores = (prob * (grad_weights - delta) * scale).astype(jnp.bfloat16)
        grad_query_parts.append(
            jnp.dot(grad_scores, key_head, preferred_element_type=jnp.float32).astype(jnp.bfloat16)
        )
        grad_key_parts.append(
            jnp.einsum("tk,ta->ka", grad_scores, query_head, preferred_element_type=jnp.float32)
        )
        grad_value_parts.append(
            jnp.einsum("tk,ta->ka", weights, grad_head, preferred_element_type=jnp.float32)
        )
    attended = jnp.concatenate(attended_parts, axis=1)
    grad_queries = jnp.concatenate(grad_query_parts, axis=1)
    grad_sets = jnp.stack(
        [jnp.concatenate(grad_key_parts, axis=1), jnp.concatenate(grad_value_parts, axis=1)]
    )
    carried = jnp.zeros((2, coarse, width), jnp.float32)
    for layer_bit in reversed(range(depth)):
        first = tokens + layer_bit * coarse
        outgoing = grad_sets[:, first : first + coarse]
        kept = jnp.zeros((2, coarse, width), jnp.float32)
        if layer_bit + 1 < depth:
            lower_half = position >> layer_bit & 1 == 0
            spread = spread_rows(carried * 0.5)
            low_part = spread[:, :coarse]
            high_part = spread[:, coarse:]
            kept = jnp.where(lower_half, low_part, high_part)
            outgoing = outgoing + jnp.where(lower_half, high_part, low_part)
        incoming = from_partner(outgoing.astype(jnp.bfloat16), SEQ, layer_bit).astype(
            outgoing.dtype
        )
        carried = kept + incoming
    own_grads = grad_sets[:, :tokens] + spread_rows(carried * 0.5)
    grad_keys = own_grads[0].astype(jnp.bfloat16)
    grad_values = own_grads[1].astype(jnp.bfloat16)
    grad_out_weight = own_rows(
        lax.dot_general(
            full_cot, attended, (((0,), (0,)), ((), ())), preferred_element_type=jnp.bfloat16
        ),
        SEQ,
    )
    return (attended, grad_queries, grad_keys, grad_values, grad_out_weight)


def solution(mesh):
    torus = Mesh(mesh.devices.reshape(8, 8, mesh.shape["dp"]), ("seq_0", "seq_1", "dp"))
    placed = (P(SEQ, "dp"), P(SEQ, "dp"), P(SEQ, "dp"), P(SEQ, "dp"), P(SEQ, "dp"))
    return jax.shard_map(
        on_device,
        mesh=torus,
        in_specs=placed,
        out_specs=(P(SEQ, "dp"), P(SEQ, "dp"), P(SEQ, "dp"), P(SEQ, "dp"), P(SEQ, "dp")),
        check_vma=False,
    )
```

```python
import math

import jax
import jax.numpy as jnp
from jax import lax
from jax.sharding import Mesh
from jax.sharding import PartitionSpec as P

HEAD = 128
SEQ = ("seq_0", "seq_1")


def from_partner(block, axis, apart):
    count = lax.axis_size(axis)
    route = []
    for low in range(count):
        high = low | 1 << apart
        if high != low and high < count:
            route += [(low, high), (high, low)]
    return lax.ppermute(block, axis, route)


def joined_along(blocks, dim):
    blocks = jnp.moveaxis(blocks, 0, dim)
    dims = blocks.shape
    return blocks.reshape(*dims[:dim], dims[dim] * dims[dim + 1], *dims[dim + 2 :])


def from_everyone(x, axis):
    copies = jnp.broadcast_to(x, (lax.axis_size(axis), *x.shape))
    return lax.all_to_all(copies, axis, split_axis=0, concat_axis=0, tiled=True)


def gathered_copies(x, axis, dim):
    return joined_along(from_everyone(x, axis), dim)


def own_rows(running, axes):
    count = lax.axis_size(axes)
    parts = running.astype(jnp.bfloat16).reshape(count, running.shape[0] // count, running.shape[1])
    return jnp.sum(lax.all_to_all(parts, axes, 0, 0, tiled=True).astype(jnp.float32), axis=0)


def pair_mean(table):
    paired = table.reshape(table.shape[0], table.shape[1] // 2, 2, table.shape[2])
    return (paired[:, :, 0] + paired[:, :, 1]) * 0.5


def spread_rows(table):
    doubled = jnp.broadcast_to(
        table[:, :, None], (table.shape[0], table.shape[1], 2, table.shape[2])
    )
    return doubled.reshape(table.shape[0], table.shape[1] * 2, table.shape[2])


def on_device(queries, keys, values, cotangent, out_weight):
    tokens = queries.shape[0]
    width = queries.shape[1]
    heads = width // HEAD
    coarse = tokens // 2
    scale = 1.0 / math.sqrt(HEAD)
    depth = lax.axis_size(SEQ).bit_length() - 1
    position = lax.axis_index(SEQ)
    rows = lax.broadcasted_iota(jnp.int32, (tokens // 2, tokens), 0)
    cols = lax.broadcasted_iota(jnp.int32, (tokens // 2, tokens), 1)
    pool = jnp.where(cols // 2 == rows, 0.5, 0.0).astype(jnp.bfloat16)
    own_table = jnp.stack(
        [
            jnp.dot(pool, keys, preferred_element_type=jnp.float32),
            jnp.dot(pool, values, preferred_element_type=jnp.float32),
        ]
    )
    far_keys = []
    far_values = []
    for layer_bit in range(depth):
        far_table = from_partner(own_table.astype(jnp.bfloat16), SEQ, layer_bit).astype(jnp.float32)
        far_keys.append(far_table[0].astype(jnp.bfloat16))
        far_values.append(far_table[1].astype(jnp.bfloat16))
        if layer_bit + 1 < depth:
            lower_half = position >> layer_bit & 1 == 0
            joined = jnp.concatenate(
                [
                    jnp.where(lower_half, own_table, far_table),
                    jnp.where(lower_half, far_table, own_table),
                ],
                axis=1,
            )
            own_table = pair_mean(joined)
    key_set = jnp.concatenate([keys] + far_keys, axis=0)
    value_set = jnp.concatenate([values] + far_values, axis=0)
    full_cot = gathered_copies(cotangent, "dp", 1)
    full_weight = gathered_copies(out_weight, SEQ, 0)
    grad_attended = jnp.dot(full_cot, full_weight, preferred_element_type=jnp.float32).astype(
        jnp.bfloat16
    )
    attended_parts = []
    grad_query_parts = []
    grad_key_parts = []
    grad_value_parts = []
    for head in range(heads):
        low = head * HEAD
        high = low + HEAD
        query_head = queries[:, low:high]
        key_head = key_set[:, low:high]
        value_head = value_set[:, low:high]
        grad_head = grad_attended[:, low:high]
        scores = (
            jnp.einsum("ta,ka->tk", query_head, key_head, preferred_element_type=jnp.float32)
            * scale
        )
        peak = jnp.max(scores, axis=-1, keepdims=True)
        expo = jnp.exp(scores - peak)
        prob = expo / jnp.sum(expo, axis=-1, keepdims=True)
        weights = prob.astype(jnp.bfloat16)
        attended_parts.append(
            jnp.dot(weights, value_head, preferred_element_type=jnp.float32).astype(jnp.bfloat16)
        )
        grad_weights = jnp.einsum(
            "ta,ka->tk", grad_head, value_head, preferred_element_type=jnp.float32
        )
        delta = jnp.sum(prob * grad_weights, axis=-1, keepdims=True)
        grad_scores = (prob * (grad_weights - delta) * scale).astype(jnp.bfloat16)
        grad_query_parts.append(
            jnp.dot(grad_scores, key_head, preferred_element_type=jnp.float32).astype(jnp.bfloat16)
        )
        grad_key_parts.append(
            jnp.einsum("tk,ta->ka", grad_scores, query_head, preferred_element_type=jnp.float32)
        )
        grad_value_parts.append(
            jnp.einsum("tk,ta->ka", weights, grad_head, preferred_element_type=jnp.float32)
        )
    attended = jnp.concatenate(attended_parts, axis=1)
    grad_queries = jnp.concatenate(grad_query_parts, axis=1)
    grad_sets = jnp.stack(
        [jnp.concatenate(grad_key_parts, axis=1), jnp.concatenate(grad_value_parts, axis=1)]
    )
    carried = jnp.zeros((2, coarse, width), jnp.float32)
    for layer_bit in reversed(range(depth)):
        first = tokens + layer_bit * coarse
        outgoing = grad_sets[:, first : first + coarse]
        kept = jnp.zeros((2, coarse, width), jnp.float32)
        if layer_bit + 1 < depth:
            lower_half = position >> layer_bit & 1 == 0
            spread = spread_rows(carried * 0.5)
            low_part = spread[:, :coarse]
            high_part = spread[:, coarse:]
            kept = jnp.where(lower_half, low_part, high_part)
            outgoing = outgoing + jnp.where(lower_half, high_part, low_part)
        incoming = from_partner(outgoing.astype(jnp.bfloat16), SEQ, layer_bit).astype(
            outgoing.dtype
        )
        carried = kept + incoming
    own_grads = grad_sets[:, :tokens] + spread_rows(carried * 0.5)
    grad_keys = own_grads[0].astype(jnp.bfloat16)
    grad_values = own_grads[1].astype(jnp.bfloat16)
    grad_out_weight = own_rows(
        lax.dot_general(
            full_cot, attended, (((0,), (0,)), ((), ())), preferred_element_type=jnp.bfloat16
        ),
        SEQ,
    )
    return (attended, grad_queries, grad_keys, grad_values, grad_out_weight)


def solution(mesh):
    torus = Mesh(mesh.devices.reshape(8, 8, mesh.shape["dp"]), ("seq_0", "seq_1", "dp"))
    placed = (P(SEQ, "dp"), P(SEQ, "dp"), P(SEQ, "dp"), P(SEQ, "dp"), P(SEQ, "dp"))
    return jax.shard_map(
        on_device,
        mesh=torus,
        in_specs=placed,
        out_specs=(P(SEQ, "dp"), P(SEQ, "dp"), P(SEQ, "dp"), P(SEQ, "dp"), P(SEQ, "dp")),
        check_vma=False,
    )
```

```python
import math

import jax
import jax.numpy as jnp
from jax import lax
from jax.sharding import Mesh
from jax.sharding import PartitionSpec as P

HEAD = 128
SEQ = ("seq_0", "seq_1")


def from_partner(block, axis, apart):
    count = lax.axis_size(axis)
    route = []
    for low in range(count):
        high = low | 1 << apart
        if high != low and high < count:
            route += [(low, high), (high, low)]
    return lax.ppermute(block, axis, route)


def joined_along(blocks, dim):
    blocks = jnp.moveaxis(blocks, 0, dim)
    dims = blocks.shape
    return blocks.reshape(*dims[:dim], dims[dim] * dims[dim + 1], *dims[dim + 2 :])


def from_everyone(x, axis):
    copies = jnp.broadcast_to(x, (lax.axis_size(axis), *x.shape))
    return lax.all_to_all(copies, axis, split_axis=0, concat_axis=0, tiled=True)


def gathered_copies(x, axis, dim):
    return joined_along(from_everyone(x, axis), dim)


def own_rows(running, axes):
    count = lax.axis_size(axes)
    parts = running.astype(jnp.bfloat16).reshape(count, running.shape[0] // count, running.shape[1])
    return jnp.sum(lax.all_to_all(parts, axes, 0, 0, tiled=True).astype(jnp.float32), axis=0)


def pair_mean(table):
    paired = table.reshape(table.shape[0], table.shape[1] // 2, 2, table.shape[2])
    return (paired[:, :, 0] + paired[:, :, 1]) * 0.5


def spread_rows(table):
    doubled = jnp.broadcast_to(
        table[:, :, None], (table.shape[0], table.shape[1], 2, table.shape[2])
    )
    return doubled.reshape(table.shape[0], table.shape[1] * 2, table.shape[2])


def on_device(queries, keys, values, cotangent, out_weight):
    tokens = queries.shape[0]
    width = queries.shape[1]
    heads = width // HEAD
    coarse = tokens // 2
    scale = 1.0 / math.sqrt(HEAD)
    depth = lax.axis_size(SEQ).bit_length() - 1
    position = lax.axis_index(SEQ)
    own_table = jnp.stack(
        [pair_mean(keys[None].astype(jnp.float32))[0], pair_mean(values[None].astype(jnp.float32))[0]]
    )
    far_keys = []
    far_values = []
    major, minor = SEQ
    minor_depth = lax.axis_size(minor).bit_length() - 1
    slice_weight = out_weight
    table_rows = 2 * coarse
    for layer_bit in range(depth):
        if layer_bit < minor_depth:
            payload = jnp.concatenate(
                [own_table.astype(jnp.bfloat16).reshape(table_rows, width), slice_weight], axis=0
            )
            got = from_partner(payload, SEQ, layer_bit)
            far_table = got[:table_rows].reshape(2, coarse, width).astype(jnp.float32)
            far_weight = got[table_rows:]
            weight_low = position >> layer_bit & 1 == 0
            slice_weight = jnp.where(
                weight_low,
                jnp.concatenate([slice_weight, far_weight], axis=0),
                jnp.concatenate([far_weight, slice_weight], axis=0),
            )
        else:
            far_table = from_partner(own_table.astype(jnp.bfloat16), SEQ, layer_bit).astype(jnp.float32)
        far_keys.append(far_table[0].astype(jnp.bfloat16))
        far_values.append(far_table[1].astype(jnp.bfloat16))
        if layer_bit + 1 < depth:
            lower_half = position >> layer_bit & 1 == 0
            joined = jnp.concatenate(
                [
                    jnp.where(lower_half, own_table, far_table),
                    jnp.where(lower_half, far_table, own_table),
                ],
                axis=1,
            )
            own_table = pair_mean(joined)
    key_set = jnp.concatenate([keys] + far_keys, axis=0)
    value_set = jnp.concatenate([values] + far_values, axis=0)
    full_cot = gathered_copies(cotangent, "dp", 1)
    full_weight = gathered_copies(slice_weight, major, 0)
    grad_attended = jnp.dot(full_cot, full_weight, preferred_element_type=jnp.float32).astype(
        jnp.bfloat16
    )
    attended_parts = []
    grad_query_parts = []
    grad_key_parts = []
    grad_value_parts = []
    for head in range(heads):
        low = head * HEAD
        high = low + HEAD
        query_head = queries[:, low:high]
        key_head = key_set[:, low:high]
        value_head = value_set[:, low:high]
        grad_head = grad_attended[:, low:high]
        scores = (
            jnp.einsum("ta,ka->tk", query_head, key_head, preferred_element_type=jnp.float32)
            * scale
        )
        peak = jnp.max(scores, axis=-1, keepdims=True)
        expo = jnp.exp(scores - peak)
        prob = expo / jnp.sum(expo, axis=-1, keepdims=True)
        weights = prob.astype(jnp.bfloat16)
        attended_parts.append(
            jnp.dot(weights, value_head, preferred_element_type=jnp.float32).astype(jnp.bfloat16)
        )
        grad_weights = jnp.einsum(
            "ta,ka->tk", grad_head, value_head, preferred_element_type=jnp.float32
        )
        delta = jnp.sum(prob * grad_weights, axis=-1, keepdims=True)
        grad_scores = (prob * (grad_weights - delta) * scale).astype(jnp.bfloat16)
        grad_query_parts.append(
            jnp.dot(grad_scores, key_head, preferred_element_type=jnp.float32).astype(jnp.bfloat16)
        )
        grad_key_parts.append(
            jnp.einsum("tk,ta->ka", grad_scores, query_head, preferred_element_type=jnp.float32)
        )
        grad_value_parts.append(
            jnp.einsum("tk,ta->ka", weights, grad_head, preferred_element_type=jnp.float32)
        )
    attended = jnp.concatenate(attended_parts, axis=1)
    grad_queries = jnp.concatenate(grad_query_parts, axis=1)
    grad_sets = jnp.stack(
        [jnp.concatenate(grad_key_parts, axis=1), jnp.concatenate(grad_value_parts, axis=1)]
    )
    carried = jnp.zeros((2, coarse, width), jnp.float32)
    for layer_bit in reversed(range(depth)):
        first = tokens + layer_bit * coarse
        outgoing = grad_sets[:, first : first + coarse]
        kept = jnp.zeros((2, coarse, width), jnp.float32)
        if layer_bit + 1 < depth:
            lower_half = position >> layer_bit & 1 == 0
            spread = spread_rows(carried * 0.5)
            low_part = spread[:, :coarse]
            high_part = spread[:, coarse:]
            kept = jnp.where(lower_half, low_part, high_part)
            outgoing = outgoing + jnp.where(lower_half, high_part, low_part)
        incoming = from_partner(outgoing.astype(jnp.bfloat16), SEQ, layer_bit).astype(
            outgoing.dtype
        )
        carried = kept + incoming
    own_grads = grad_sets[:, :tokens] + spread_rows(carried * 0.5)
    grad_keys = own_grads[0].astype(jnp.bfloat16)
    grad_values = own_grads[1].astype(jnp.bfloat16)
    grad_out_weight = own_rows(
        lax.dot_general(
            full_cot, attended, (((0,), (0,)), ((), ())), preferred_element_type=jnp.bfloat16
        ),
        SEQ,
    )
    return (attended, grad_queries, grad_keys, grad_values, grad_out_weight)


def solution(mesh):
    torus = Mesh(mesh.devices.reshape(8, 8, mesh.shape["dp"]), ("seq_0", "seq_1", "dp"))
    placed = (P(SEQ, "dp"), P(SEQ, "dp"), P(SEQ, "dp"), P(SEQ, "dp"), P(SEQ, "dp"))
    return jax.shard_map(
        on_device,
        mesh=torus,
        in_specs=placed,
        out_specs=(P(SEQ, "dp"), P(SEQ, "dp"), P(SEQ, "dp"), P(SEQ, "dp"), P(SEQ, "dp")),
        check_vma=False,
    )
```

```python
import math

import jax
import jax.numpy as jnp
from jax import lax
from jax.sharding import Mesh
from jax.sharding import PartitionSpec as P

HEAD = 128
SEQ = ("seq_0", "seq_1")


def from_partner(block, axis, apart):
    count = lax.axis_size(axis)
    route = []
    for low in range(count):
        high = low | 1 << apart
        if high != low and high < count:
            route += [(low, high), (high, low)]
    return lax.ppermute(block, axis, route)


def joined_along(blocks, dim):
    blocks = jnp.moveaxis(blocks, 0, dim)
    dims = blocks.shape
    return blocks.reshape(*dims[:dim], dims[dim] * dims[dim + 1], *dims[dim + 2 :])


def from_everyone(x, axis):
    copies = jnp.broadcast_to(x, (lax.axis_size(axis), *x.shape))
    return lax.all_to_all(copies, axis, split_axis=0, concat_axis=0, tiled=True)


def gathered_copies(x, axis, dim):
    return joined_along(from_everyone(x, axis), dim)


def own_rows(running, axes):
    count = lax.axis_size(axes)
    parts = running.astype(jnp.bfloat16).reshape(count, running.shape[0] // count, running.shape[1])
    return jnp.sum(lax.all_to_all(parts, axes, 0, 0, tiled=True).astype(jnp.float32), axis=0)


def pair_mean(table):
    paired = table.reshape(table.shape[0], table.shape[1] // 2, 2, table.shape[2])
    return (paired[:, :, 0] + paired[:, :, 1]) * 0.5


def spread_rows(table):
    doubled = jnp.broadcast_to(
        table[:, :, None], (table.shape[0], table.shape[1], 2, table.shape[2])
    )
    return doubled.reshape(table.shape[0], table.shape[1] * 2, table.shape[2])


def on_device(queries, keys, values, cotangent, out_weight):
    tokens = queries.shape[0]
    width = queries.shape[1]
    heads = width // HEAD
    coarse = tokens // 2
    scale = 1.0 / math.sqrt(HEAD)
    depth = lax.axis_size(SEQ).bit_length() - 1
    position = lax.axis_index(SEQ)
    own_table = jnp.stack(
        [pair_mean(keys[None].astype(jnp.float32))[0], pair_mean(values[None].astype(jnp.float32))[0]]
    )
    far_keys = []
    far_values = []
    major, minor = SEQ
    minor_depth = lax.axis_size(minor).bit_length() - 1
    slice_weight = out_weight
    table_rows = 2 * coarse
    for layer_bit in range(depth):
        if layer_bit < minor_depth:
            payload = jnp.concatenate(
                [own_table.astype(jnp.bfloat16).reshape(table_rows, width), slice_weight], axis=0
            )
            got = from_partner(payload, SEQ, layer_bit)
            far_table = got[:table_rows].reshape(2, coarse, width).astype(jnp.float32)
            far_weight = got[table_rows:]
            weight_low = position >> layer_bit & 1 == 0
            slice_weight = jnp.where(
                weight_low,
                jnp.concatenate([slice_weight, far_weight], axis=0),
                jnp.concatenate([far_weight, slice_weight], axis=0),
            )
        else:
            far_table = from_partner(own_table.astype(jnp.bfloat16), SEQ, layer_bit).astype(jnp.float32)
        far_keys.append(far_table[0].astype(jnp.bfloat16))
        far_values.append(far_table[1].astype(jnp.bfloat16))
        if layer_bit + 1 < depth:
            lower_half = position >> layer_bit & 1 == 0
            joined = jnp.concatenate(
                [
                    jnp.where(lower_half, own_table, far_table),
                    jnp.where(lower_half, far_table, own_table),
                ],
                axis=1,
            )
            own_table = pair_mean(joined)
    key_set = jnp.concatenate([keys] + far_keys, axis=0)
    value_set = jnp.concatenate([values] + far_values, axis=0)
    full_cot = gathered_copies(cotangent, "dp", 1)
    full_weight = gathered_copies(slice_weight, major, 0)
    grad_attended = jnp.dot(full_cot, full_weight, preferred_element_type=jnp.float32).astype(
        jnp.bfloat16
    )
    attended_parts = []
    grad_query_parts = []
    grad_key_parts = []
    grad_value_parts = []
    for head in range(heads):
        low = head * HEAD
        high = low + HEAD
        query_head = queries[:, low:high]
        key_head = key_set[:, low:high]
        value_head = value_set[:, low:high]
        grad_head = grad_attended[:, low:high]
        scores = (
            jnp.einsum("ta,ka->tk", query_head, key_head, preferred_element_type=jnp.float32)
            * scale
        )
        peak = jnp.max(scores, axis=-1, keepdims=True)
        expo = jnp.exp(scores - peak)
        prob = expo / jnp.sum(expo, axis=-1, keepdims=True)
        weights = prob.astype(jnp.bfloat16)
        attended_parts.append(
            jnp.dot(weights, value_head, preferred_element_type=jnp.float32).astype(jnp.bfloat16)
        )
        grad_weights = jnp.einsum(
            "ta,ka->tk", grad_head, value_head, preferred_element_type=jnp.float32
        )
        delta = jnp.sum(prob * grad_weights, axis=-1, keepdims=True)
        grad_scores = (prob * (grad_weights - delta) * scale).astype(jnp.bfloat16)
        grad_query_parts.append(
            jnp.dot(grad_scores, key_head, preferred_element_type=jnp.float32).astype(jnp.bfloat16)
        )
        grad_key_parts.append(
            jnp.einsum("tk,ta->ka", grad_scores, query_head, preferred_element_type=jnp.float32)
        )
        grad_value_parts.append(
            jnp.einsum("tk,ta->ka", weights, grad_head, preferred_element_type=jnp.float32)
        )
    attended = jnp.concatenate(attended_parts, axis=1)
    grad_queries = jnp.concatenate(grad_query_parts, axis=1)
    grad_sets = jnp.stack(
        [jnp.concatenate(grad_key_parts, axis=1), jnp.concatenate(grad_value_parts, axis=1)]
    )
    weight_grad = lax.dot_general(
        full_cot, attended, (((0,), (0,)), ((), ())), preferred_element_type=jnp.bfloat16
    )
    n_major = lax.axis_size(major)
    weight_grad = lax.all_to_all(
        weight_grad.reshape(n_major, weight_grad.shape[0] // n_major, width), major, 0, 0, tiled=True
    )
    weight_sum = jnp.sum(weight_grad.astype(jnp.float32), axis=0)
    carried = jnp.zeros((2, coarse, width), jnp.float32)
    for layer_bit in reversed(range(depth)):
        first = tokens + layer_bit * coarse
        outgoing = grad_sets[:, first : first + coarse]
        kept = jnp.zeros((2, coarse, width), jnp.float32)
        if layer_bit + 1 < depth:
            lower_half = position >> layer_bit & 1 == 0
            spread = spread_rows(carried * 0.5)
            low_part = spread[:, :coarse]
            high_part = spread[:, coarse:]
            kept = jnp.where(lower_half, low_part, high_part)
            outgoing = outgoing + jnp.where(lower_half, high_part, low_part)
        if layer_bit < minor_depth:
            half = weight_sum.shape[0] // 2
            weight_low = position >> layer_bit & 1 == 0
            keep_w = jnp.where(weight_low, weight_sum[:half], weight_sum[half:])
            send_w = jnp.where(weight_low, weight_sum[half:], weight_sum[:half])
            payload = jnp.concatenate(
                [outgoing.astype(jnp.bfloat16).reshape(2 * coarse, width), send_w.astype(jnp.bfloat16)], axis=0
            )
            got = from_partner(payload, SEQ, layer_bit)
            incoming = got[: 2 * coarse].reshape(2, coarse, width).astype(outgoing.dtype)
            weight_sum = keep_w + got[2 * coarse :].astype(jnp.float32)
        else:
            incoming = from_partner(outgoing.astype(jnp.bfloat16), SEQ, layer_bit).astype(
                outgoing.dtype
            )
        carried = kept + incoming
    own_grads = grad_sets[:, :tokens] + spread_rows(carried * 0.5)
    grad_keys = own_grads[0].astype(jnp.bfloat16)
    grad_values = own_grads[1].astype(jnp.bfloat16)
    grad_out_weight = weight_sum
    return (attended, grad_queries, grad_keys, grad_values, grad_out_weight)


def solution(mesh):
    torus = Mesh(mesh.devices.reshape(8, 8, mesh.shape["dp"]), ("seq_0", "seq_1", "dp"))
    placed = (P(SEQ, "dp"), P(SEQ, "dp"), P(SEQ, "dp"), P(SEQ, "dp"), P(SEQ, "dp"))
    return jax.shard_map(
        on_device,
        mesh=torus,
        in_specs=placed,
        out_specs=(P(SEQ, "dp"), P(SEQ, "dp"), P(SEQ, "dp"), P(SEQ, "dp"), P(SEQ, "dp")),
        check_vma=False,
    )
```

```python
import math

import jax
import jax.numpy as jnp
from jax import lax
from jax.sharding import Mesh
from jax.sharding import PartitionSpec as P

HEAD = 128
SEQ = ("seq_0", "seq_1")


def from_partner(block, axis, apart):
    count = lax.axis_size(axis)
    route = []
    for low in range(count):
        high = low | 1 << apart
        if high != low and high < count:
            route += [(low, high), (high, low)]
    return lax.ppermute(block, axis, route)


def joined_along(blocks, dim):
    blocks = jnp.moveaxis(blocks, 0, dim)
    dims = blocks.shape
    return blocks.reshape(*dims[:dim], dims[dim] * dims[dim + 1], *dims[dim + 2 :])


def from_everyone(x, axis):
    copies = jnp.broadcast_to(x, (lax.axis_size(axis), *x.shape))
    return lax.all_to_all(copies, axis, split_axis=0, concat_axis=0, tiled=True)


def gathered_copies(x, axis, dim):
    return joined_along(from_everyone(x, axis), dim)


def own_rows(running, axes):
    major, minor = axes
    n_major = lax.axis_size(major)
    n_minor = lax.axis_size(minor)
    rows = running.shape[0] // (n_major * n_minor)
    parts = running.astype(jnp.bfloat16).reshape(n_major, n_minor, rows, running.shape[1])
    parts = jnp.moveaxis(parts, 1, 0)
    summed = jnp.sum(lax.all_to_all(parts, minor, 0, 0, tiled=True).astype(jnp.float32), axis=0)
    return jnp.sum(lax.all_to_all(summed.astype(jnp.bfloat16), major, 0, 0, tiled=True).astype(jnp.float32), axis=0)


def pair_mean(table):
    paired = table.reshape(table.shape[0], table.shape[1] // 2, 2, table.shape[2])
    return (paired[:, :, 0] + paired[:, :, 1]) * 0.5


def spread_rows(table):
    doubled = jnp.broadcast_to(
        table[:, :, None], (table.shape[0], table.shape[1], 2, table.shape[2])
    )
    return doubled.reshape(table.shape[0], table.shape[1] * 2, table.shape[2])


def on_device(queries, keys, values, cotangent, out_weight):
    tokens = queries.shape[0]
    width = queries.shape[1]
    heads = width // HEAD
    coarse = tokens // 2
    scale = 1.0 / math.sqrt(HEAD)
    depth = lax.axis_size(SEQ).bit_length() - 1
    position = lax.axis_index(SEQ)
    own_table = jnp.stack(
        [pair_mean(keys[None].astype(jnp.float32))[0], pair_mean(values[None].astype(jnp.float32))[0]]
    )
    far_keys = []
    far_values = []
    major, minor = SEQ
    minor_depth = lax.axis_size(minor).bit_length() - 1
    slice_weight = out_weight
    table_rows = 2 * coarse
    for layer_bit in range(depth):
        if layer_bit < minor_depth:
            payload = jnp.concatenate(
                [own_table.astype(jnp.bfloat16).reshape(table_rows, width), slice_weight], axis=0
            )
            got = from_partner(payload, SEQ, layer_bit)
            far_table = got[:table_rows].reshape(2, coarse, width).astype(jnp.float32)
            far_weight = got[table_rows:]
            weight_low = position >> layer_bit & 1 == 0
            slice_weight = jnp.where(
                weight_low,
                jnp.concatenate([slice_weight, far_weight], axis=0),
                jnp.concatenate([far_weight, slice_weight], axis=0),
            )
        else:
            far_table = from_partner(own_table.astype(jnp.bfloat16), SEQ, layer_bit).astype(jnp.float32)
        far_keys.append(far_table[0].astype(jnp.bfloat16))
        far_values.append(far_table[1].astype(jnp.bfloat16))
        if layer_bit + 1 < depth:
            lower_half = position >> layer_bit & 1 == 0
            joined = jnp.concatenate(
                [
                    jnp.where(lower_half, own_table, far_table),
                    jnp.where(lower_half, far_table, own_table),
                ],
                axis=1,
            )
            own_table = pair_mean(joined)
    key_set = jnp.concatenate([keys] + far_keys, axis=0)
    value_set = jnp.concatenate([values] + far_values, axis=0)
    full_cot = gathered_copies(cotangent, "dp", 1)
    full_weight = gathered_copies(slice_weight, major, 0)
    grad_attended = jnp.dot(full_cot, full_weight, preferred_element_type=jnp.float32).astype(
        jnp.bfloat16
    )
    attended_parts = []
    grad_query_parts = []
    grad_key_parts = []
    grad_value_parts = []
    for head in range(heads):
        low = head * HEAD
        high = low + HEAD
        query_head = queries[:, low:high]
        key_head = key_set[:, low:high]
        value_head = value_set[:, low:high]
        grad_head = grad_attended[:, low:high]
        scores = (
            jnp.einsum("ta,ka->tk", query_head, key_head, preferred_element_type=jnp.float32)
            * scale
        )
        peak = jnp.max(scores, axis=-1, keepdims=True)
        expo = jnp.exp(scores - peak)
        prob = expo / jnp.sum(expo, axis=-1, keepdims=True)
        weights = prob.astype(jnp.bfloat16)
        attended_parts.append(
            jnp.dot(weights, value_head, preferred_element_type=jnp.float32).astype(jnp.bfloat16)
        )
        grad_weights = jnp.einsum(
            "ta,ka->tk", grad_head, value_head, preferred_element_type=jnp.float32
        )
        delta = jnp.sum(prob * grad_weights, axis=-1, keepdims=True)
        grad_scores = (prob * (grad_weights - delta) * scale).astype(jnp.bfloat16)
        grad_query_parts.append(
            jnp.dot(grad_scores, key_head, preferred_element_type=jnp.float32).astype(jnp.bfloat16)
        )
        grad_key_parts.append(
            jnp.einsum("tk,ta->ka", grad_scores, query_head, preferred_element_type=jnp.float32)
        )
        grad_value_parts.append(
            jnp.einsum("tk,ta->ka", weights, grad_head, preferred_element_type=jnp.float32)
        )
    attended = jnp.concatenate(attended_parts, axis=1)
    grad_queries = jnp.concatenate(grad_query_parts, axis=1)
    grad_sets = jnp.stack(
        [jnp.concatenate(grad_key_parts, axis=1), jnp.concatenate(grad_value_parts, axis=1)]
    )
    carried = jnp.zeros((2, coarse, width), jnp.float32)
    for layer_bit in reversed(range(depth)):
        first = tokens + layer_bit * coarse
        outgoing = grad_sets[:, first : first + coarse]
        kept = jnp.zeros((2, coarse, width), jnp.float32)
        if layer_bit + 1 < depth:
            lower_half = position >> layer_bit & 1 == 0
            spread = spread_rows(carried * 0.5)
            low_part = spread[:, :coarse]
            high_part = spread[:, coarse:]
            kept = jnp.where(lower_half, low_part, high_part)
            outgoing = outgoing + jnp.where(lower_half, high_part, low_part)
        incoming = from_partner(outgoing.astype(jnp.bfloat16), SEQ, layer_bit).astype(
            outgoing.dtype
        )
        carried = kept + incoming
    own_grads = grad_sets[:, :tokens] + spread_rows(carried * 0.5)
    grad_keys = own_grads[0].astype(jnp.bfloat16)
    grad_values = own_grads[1].astype(jnp.bfloat16)
    grad_out_weight = own_rows(
        lax.dot_general(
            full_cot, attended, (((0,), (0,)), ((), ())), preferred_element_type=jnp.bfloat16
        ),
        SEQ,
    )
    return (attended, grad_queries, grad_keys, grad_values, grad_out_weight)


def solution(mesh):
    torus = Mesh(mesh.devices.reshape(8, 8, mesh.shape["dp"]), ("seq_0", "seq_1", "dp"))
    placed = (P(SEQ, "dp"), P(SEQ, "dp"), P(SEQ, "dp"), P(SEQ, "dp"), P(SEQ, "dp"))
    return jax.shard_map(
        on_device,
        mesh=torus,
        in_specs=placed,
        out_specs=(P(SEQ, "dp"), P(SEQ, "dp"), P(SEQ, "dp"), P(SEQ, "dp"), P(SEQ, "dp")),
        check_vma=False,
    )
```
